32 devices in a mesh: node: 8 (over z, x), fsdp: 4 (over y, core).
Axes of the slice: x: 2, y: 2, z: 4, core: 2. Of those that a mesh axis runs over, the one named last changes fastest.
Arguments:
- feature_table: bfloat16 [32768, 1024], P(('node', 'fsdp')), may hold values from -6 to 6
- vertex_labels: int32 [96, 256], P(('node', 'fsdp')), may hold values from 0 to 32767, as said below
- incidence_mask: int32 [96, 256, 256], P(('node', 'fsdp')), may hold values 0 or 1
- weight_one: bfloat16 [1024, 1024], P(None, 'fsdp'), may hold values from -0.1875 to 0.1875
- weight_two: bfloat16 [1024, 1024], P(None, 'fsdp'), may hold values from -0.1875 to 0.1875
- final_layer_sensitivity: bfloat16 [96, 256, 1024], P(('node', 'fsdp')), may hold values from -6 to 6
Outputs:
- embedding_matrix_sensitivity: float32 [32768, 1024], P(('node', 'fsdp'))
- grad_one: float32 [1024, 1024], P(None, ('node', 'fsdp'))
- grad_two: float32 [1024, 1024], P(None, ('node', 'fsdp'))
The draws below stay inside these ranges and needn't reach their ends.
Inputs may be any that keep to these rules, and one draw needn't show every extreme that they name: `vertex_labels`: id k lies in the table rows of device k // 1024, devices numbered with node as the slower index. Among the ids of one device's 3 subgraphs, at most 49 lie in the rows of any one device; in every such block some device's rows receive exactly 49, and one device's rows receive exactly 49 from every block.
All inputs are finite; a program needn't handle non-finite values. No bound on the sum of `incidence_mask` on one device may be relied on, other than what follows from the above.
Results may differ from the reference program's by a relative error of at most 0.008.
Values may be sent and summed in bfloat16 or wider, within the bound.
No kernel may reach another device: no remote copies, remote signals or barrier semaphores. Data moves between devices by JAX's collectives and lax.ppermute only.
A program may use at most 128 MiB of HBM per device.

```python
import jax
import jax.numpy as jnp
from jax import lax

EMBED_BREADTH = 1024
VERTICES_PER_HOOD = 256
LOCAL_NEIGHBORHOODS = 3
ROWS_DEV = 1024
GLOBAL_HOODS = 96
NODES = 32768
CAP = 49
DEVICES = 32


def draw_vertex_labels(key, part):
    total_slots = DEVICES * CAP
    selected_entries = LOCAL_NEIGHBORHOODS * VERTICES_PER_HOOD
    common = jax.random.randint(jax.random.fold_in(key, 11), (), 0, DEVICES)
    slot_owner = jnp.arange(total_slots, dtype=jnp.int32) // CAP

    def one_block(index):
        block_key = jax.random.fold_in(jax.random.fold_in(key, 12), index)
        chosen_owner = jax.random.randint(jax.random.fold_in(block_key, 1), (), 0, DEVICES)
        priority = jax.random.permutation(jax.random.fold_in(block_key, 2), total_slots).astype(jnp.int32)
        forced = jnp.logical_or(slot_owner == common, slot_owner == chosen_owner).astype(jnp.int32)
        priority = priority - forced * total_slots
        order = jnp.argsort(priority, stable=True)[:selected_entries]
        mixing = jax.random.permutation(jax.random.fold_in(block_key, 3), selected_entries)
        owners = slot_owner[order][mixing]
        local_rows = jax.random.randint(jax.random.fold_in(block_key, 4), (selected_entries,), 0, ROWS_DEV)
        return (owners * ROWS_DEV + local_rows).astype(jnp.int32)
    section_sequence = jax.vmap(one_block)(jnp.arange(DEVICES, dtype=jnp.int32))
    return section_sequence.reshape(DEVICES * LOCAL_NEIGHBORHOODS, VERTICES_PER_HOOD)


def place_ends(values, key, smallest, top_value):
    longest = values.shape.index(max(values.shape))
    spots = []
    for shift in (0, 1):
        where = [jax.random.randint(jax.random.fold_in(key, axis), (), 0, length) for axis, length in enumerate(values.shape)]
        where[longest] = (where[longest] + shift) % values.shape[longest]
        spots.append(tuple(where))
    return values.at[spots[0]].set(smallest).at[spots[1]].set(top_value)


def with_spikes(drawn, rng, source, target, parts, factor):
    owner, partner = [(jnp.arange(drawn.shape[position]) // (drawn.shape[position] // parts)).reshape([-1 if axis == position else 1 for axis in range(drawn.ndim)]) for position in (source, target)]
    chosen = jax.random.permutation(rng, parts)[partner]
    strong = (owner == chosen) | (owner == (partner + parts // 2) % parts)
    return jnp.where(strong, factor * drawn, drawn)


def steps_of(rng, extent, pieces, smallest, largest):
    gain, own = 1.0, jax.random.fold_in(rng, 6)
    for dim, parts in pieces:
        heights = jnp.exp(jax.random.uniform(jax.random.fold_in(own, dim), (parts,), jnp.float32, smallest / len(pieces), largest / len(pieces)))
        gain = gain * jnp.repeat(heights, extent[dim] // parts).reshape([-1 if axis == dim else 1 for axis in range(len(extent))])
    return gain


def scatter_about(stream_key, extent, deviation, bound, split=(), kind=jnp.bfloat16):
    entries = jax.random.normal(stream_key, extent, jnp.float32) * deviation
    if len(split) > 0:
        entries = steps_of(stream_key, extent, split, -0.22, 0.18) * entries
    return jnp.clip(entries, min=-bound, max=bound).astype(kind)


def noise_with(key, extent, scale, most, split, heavy, kind=jnp.bfloat16):
    values = scale * jax.random.normal(key, extent, jnp.float32)
    if split:
        values = values * steps_of(key, extent, split, -0.22, 0.18)
    return jnp.clip(with_spikes(values, jax.random.fold_in(key, 3), *heavy), -most, most).astype(kind)


def setup_inputs(seed: int = 0) -> dict:
    arg_keys = jax.random.split(jax.random.key(seed), 7)
    feature_table = scatter_about(arg_keys[0], (NODES, EMBED_BREADTH), 1.0, 6.0, ((0, 32),))
    vertex_labels = draw_vertex_labels(jax.random.fold_in(arg_keys[6], 71), 0)
    incidence_mask = place_ends((jax.random.randint(arg_keys[2], (GLOBAL_HOODS, VERTICES_PER_HOOD, VERTICES_PER_HOOD), 0, 8) < 1).astype(jnp.int32), jax.random.fold_in(arg_keys[2], 1), 0, 1)
    weight_one = scatter_about(arg_keys[3], (EMBED_BREADTH, EMBED_BREADTH), EMBED_BREADTH ** -0.5, 0.1875, ((1, 4),))
    weight_two = scatter_about(arg_keys[4], (EMBED_BREADTH, EMBED_BREADTH), EMBED_BREADTH ** -0.5, 0.1875, ((1, 4),))
    final_layer_sensitivity = noise_with(arg_keys[5], (GLOBAL_HOODS, VERTICES_PER_HOOD, EMBED_BREADTH), 1.0, 6.0, ((0, 32),), (0, 2, 32, 2.75))
    return {"feature_table": feature_table, "vertex_labels": vertex_labels, "incidence_mask": incidence_mask, "weight_one": weight_one, "weight_two": weight_two, "final_layer_sensitivity": final_layer_sensitivity}


def swish_slope(values):
    sigma = jax.nn.sigmoid(values)
    return sigma * (1.0 + values * (1.0 - sigma))

def spread(link, values):
    return jnp.einsum('gij,gjd->gid', link.astype(jnp.float32), values.astype(jnp.float32))

def spread_back(link, values):
    return jnp.einsum('gji,gjd->gid', link.astype(jnp.float32), values.astype(jnp.float32))

def reference(feature_table, vertex_labels, incidence_mask, weight_one, weight_two, final_layer_sensitivity):
    section_sequence = GLOBAL_HOODS // LOCAL_NEIGHBORHOODS
    lookup_records = LOCAL_NEIGHBORHOODS * VERTICES_PER_HOOD
    vertex_label_pieces = vertex_labels.reshape(section_sequence, LOCAL_NEIGHBORHOODS, VERTICES_PER_HOOD)
    linkage_pieces = incidence_mask.reshape(section_sequence, LOCAL_NEIGHBORHOODS, VERTICES_PER_HOOD, VERTICES_PER_HOOD)
    sensitivity_pieces = final_layer_sensitivity.reshape(section_sequence, LOCAL_NEIGHBORHOODS, VERTICES_PER_HOOD, EMBED_BREADTH)
    unit_matrix = jnp.eye(VERTICES_PER_HOOD, dtype=jnp.int32)

    def step(carry, block):
        ids, adj, cot = block
        normalizer_factor = lax.rsqrt(1.0 + lax.optimization_barrier(jnp.sum(adj, axis=2)).astype(jnp.float32))[..., None]
        link = (adj + unit_matrix[None]).astype(jnp.bfloat16)
        feats = feature_table[ids]
        mixed_one = (normalizer_factor * spread(link, feats)).astype(jnp.bfloat16).reshape(lookup_records, EMBED_BREADTH)
        first_matmul_result = jnp.dot(mixed_one, weight_one, preferred_element_type=jnp.float32)
        latent_state = jax.nn.silu(first_matmul_result).astype(jnp.bfloat16).reshape(LOCAL_NEIGHBORHOODS, VERTICES_PER_HOOD, EMBED_BREADTH)
        mixed_two = (normalizer_factor * spread(link, latent_state)).astype(jnp.bfloat16).reshape(lookup_records, EMBED_BREADTH)
        product_two = jnp.dot(mixed_two, weight_two, preferred_element_type=jnp.float32)
        delta_two = (cot.reshape(lookup_records, EMBED_BREADTH).astype(jnp.float32) * swish_slope(product_two)).astype(jnp.bfloat16)
        grad_two = jnp.dot(mixed_two.T, delta_two, preferred_element_type=jnp.float32)
        upstream_second = jnp.dot(delta_two, weight_two.T, preferred_element_type=jnp.float32)
        fetched_second = (normalizer_factor * upstream_second.reshape(LOCAL_NEIGHBORHOODS, VERTICES_PER_HOOD, EMBED_BREADTH)).astype(jnp.bfloat16)
        delta_one = (spread_back(link, fetched_second).reshape(lookup_records, EMBED_BREADTH) * swish_slope(first_matmul_result)).astype(jnp.bfloat16)
        grad_one = jnp.dot(mixed_one.T, delta_one, preferred_element_type=jnp.float32)
        upstream_first = jnp.dot(delta_one, weight_one.T, preferred_element_type=jnp.float32)
        fetched_first = (normalizer_factor * upstream_first.reshape(LOCAL_NEIGHBORHOODS, VERTICES_PER_HOOD, EMBED_BREADTH)).astype(jnp.bfloat16)
        input_grad = spread_back(link, fetched_first).astype(jnp.bfloat16)
        return ((carry[0] + grad_one, carry[1] + grad_two), input_grad)
    zeros = jnp.zeros((EMBED_BREADTH, EMBED_BREADTH), jnp.float32)
    running_totals, input_grads = lax.scan(step, (zeros, zeros), (vertex_label_pieces, linkage_pieces, sensitivity_pieces))
    embedding_matrix_sensitivity = jnp.zeros((NODES, EMBED_BREADTH), jnp.float32).at[vertex_labels.reshape(-1)].add(input_grads.reshape(-1, EMBED_BREADTH).astype(jnp.float32))
    return (embedding_matrix_sensitivity, running_totals[0] / GLOBAL_HOODS, running_totals[1] / GLOBAL_HOODS)
```

```python
import jax
import jax.numpy as jnp
from jax import lax
from jax.sharding import PartitionSpec as P

AXES = ("node", "fsdp")


def swish_slope(values):
    sigma = jax.nn.sigmoid(values)
    return sigma * (1.0 + values * (1.0 - sigma))


def spread(link, values):
    return jnp.einsum("gij,gjd->gid", link, values, preferred_element_type=jnp.float32)


def spread_back(link, values):
    return jnp.einsum("gji,gjd->gid", link, values, preferred_element_type=jnp.float32)


def exchange(values):
    return lax.all_to_all(values, AXES, 0, 0, tiled=True)


def on_device(
    feature_table, vertex_labels, incidence_mask, weight_one, weight_two, final_layer_sensitivity
):
    groups, width = vertex_labels.shape
    count = groups * width
    n_node = lax.axis_size("node")
    n_fsdp = lax.axis_size("fsdp")
    shards = n_node * n_fsdp
    rows_here = feature_table.shape[0]
    depth = feature_table.shape[1]
    capacity = (2 * count + shards - 1) // shards + 1
    slots = shards * capacity
    flat_ids = vertex_labels.reshape(count)
    owner = flat_ids // rows_here
    within = flat_ids % rows_here
    one_hot = (owner[:, None] == jnp.arange(shards, dtype=jnp.int32)[None, :]).astype(jnp.int32)
    before = jnp.cumsum(one_hot, axis=0) - one_hot
    rank = jnp.sum(before * one_hot, axis=1)
    position = owner * capacity + rank
    requests = jnp.full((slots,), -1, jnp.int32).at[position].set(within)
    asked = exchange(requests)
    valid = asked >= 0
    safe_rows = jnp.maximum(asked, 0)
    found = feature_table[safe_rows] * valid[:, None].astype(jnp.bfloat16)
    answered = exchange(found)
    inputs = answered[position].reshape(groups, width, depth)
    degree = jnp.sum(incidence_mask, axis=2).astype(jnp.float32)
    normalizer_factor = lax.rsqrt(1.0 + degree)[..., None]
    link = (incidence_mask + jnp.eye(width, dtype=jnp.int32)[None]).astype(jnp.bfloat16)

    def forward_layer(layer_in, weight):
        mixed = (
            (normalizer_factor * spread(link, layer_in)).astype(jnp.bfloat16).reshape(count, depth)
        )
        product = jnp.dot(
            mixed,
            lax.all_gather(weight, "fsdp", axis=1, tiled=True),
            preferred_element_type=jnp.float32,
        )
        return (mixed, product, weight)

    def back_weight(delta, weight):
        return lax.dot_general(
            delta,
            lax.all_gather(weight, "fsdp", axis=1, tiled=True),
            (((1,), (1,)), ((), ())),
            preferred_element_type=jnp.float32,
        )

    def weight_grad(mixed, delta):
        summed = lax.psum_scatter(
            lax.dot_general(
                delta, mixed, (((0,), (0,)), ((), ())), preferred_element_type=jnp.float32
            ),
            AXES,
            scatter_dimension=0,
            tiled=True,
        )
        return (summed / (groups * shards)).T

    mixed_one, first_matmul_result, whole_one = forward_layer(inputs, weight_one)
    latent_state = (
        jax.nn.silu(first_matmul_result).astype(jnp.bfloat16).reshape(groups, width, depth)
    )
    mixed_two, product_two, whole_two = forward_layer(latent_state, weight_two)
    delta_two = (
        final_layer_sensitivity.reshape(count, depth).astype(jnp.float32) * swish_slope(product_two)
    ).astype(jnp.bfloat16)
    grad_two = weight_grad(mixed_two, delta_two)
    upstream_second = back_weight(delta_two, weight_two)
    fetched_second = (normalizer_factor * upstream_second.reshape(groups, width, depth)).astype(
        jnp.bfloat16
    )
    delta_one = (
        spread_back(link, fetched_second).reshape(count, depth) * swish_slope(first_matmul_result)
    ).astype(jnp.bfloat16)
    grad_one = weight_grad(mixed_one, delta_one)
    upstream_first = back_weight(delta_one, weight_one)
    fetched_first = (normalizer_factor * upstream_first.reshape(groups, width, depth)).astype(
        jnp.bfloat16
    )
    input_grad = spread_back(link, fetched_first).astype(jnp.bfloat16).reshape(count, depth)
    source = jnp.full((slots,), count, jnp.int32).at[position].set(
        jnp.arange(count, dtype=jnp.int32)
    )
    padded = jnp.concatenate([input_grad, jnp.zeros((1, depth), jnp.bfloat16)], axis=0)
    returned = exchange(padded[source])
    picks = (
        (safe_rows[:, None] == jnp.arange(rows_here, dtype=jnp.int32)[None, :]) & valid[:, None]
    ).astype(jnp.bfloat16)
    table_grad = lax.dot_general(
        picks, returned, (((0,), (0,)), ((), ())), preferred_element_type=jnp.float32
    )
    return (table_grad, grad_one, grad_two)


def solution(mesh):
    placed = (
        P(AXES, None),
        P(AXES, None),
        P(AXES, None, None),
        P(None, "fsdp"),
        P(None, "fsdp"),
        P(AXES, None, None),
    )
    return jax.shard_map(
        on_device,
        mesh=mesh,
        in_specs=placed,
        out_specs=(P(AXES, None), P(None, AXES), P(None, AXES)),
        check_vma=False,
    )
```

```python
import jax
import jax.numpy as jnp
from jax import lax
from jax.sharding import PartitionSpec as P

AXES = ("node", "fsdp")


def swish_slope(values):
    sigma = jax.nn.sigmoid(values)
    return sigma * (1.0 + values * (1.0 - sigma))


def spread(link, values):
    return jnp.einsum("gij,gjd->gid", link, values, preferred_element_type=jnp.float32)


def spread_back(link, values):
    return jnp.einsum("gji,gjd->gid", link, values, preferred_element_type=jnp.float32)


def exchange(values):
    return lax.all_to_all(values, AXES, 0, 0, tiled=True)


def on_device(
    feature_table, vertex_labels, incidence_mask, weight_one, weight_two, final_layer_sensitivity
):
    groups, width = vertex_labels.shape
    count = groups * width
    n_node = lax.axis_size("node")
    n_fsdp = lax.axis_size("fsdp")
    shards = n_node * n_fsdp
    rows_here = feature_table.shape[0]
    depth = feature_table.shape[1]
    capacity = (2 * count + shards - 1) // shards + 1
    flat_ids = vertex_labels.reshape(count)
    owner = flat_ids // rows_here
    within = flat_ids % rows_here
    one_hot = (owner[:, None] == jnp.arange(shards, dtype=jnp.int32)[None, :]).astype(jnp.int32)
    before = jnp.cumsum(one_hot, axis=0) - one_hot
    rank = jnp.sum(before * one_hot, axis=1)
    requests = jnp.full((shards, capacity), -1, jnp.int32).at[owner, rank].set(within)
    asked = exchange(requests)
    valid = asked >= 0
    safe_rows = jnp.maximum(asked, 0)
    found = feature_table[safe_rows] * valid[..., None].astype(jnp.bfloat16)
    answered = exchange(found)
    inputs = answered[owner, rank].reshape(groups, width, depth)
    degree = jnp.sum(incidence_mask, axis=2).astype(jnp.float32)
    normalizer_factor = lax.rsqrt(1.0 + degree)[..., None]
    link = (incidence_mask + jnp.eye(width, dtype=jnp.int32)[None]).astype(jnp.bfloat16)

    def forward_layer(layer_in, weight):
        mixed = (
            (normalizer_factor * spread(link, layer_in)).astype(jnp.bfloat16).reshape(count, depth)
        )
        product = jnp.dot(
            mixed,
            lax.all_gather(weight, "fsdp", axis=1, tiled=True),
            preferred_element_type=jnp.float32,
        )
        return (mixed, product, weight)

    def back_weight(delta, weight):
        return lax.dot_general(
            delta,
            lax.all_gather(weight, "fsdp", axis=1, tiled=True),
            (((1,), (1,)), ((), ())),
            preferred_element_type=jnp.float32,
        )

    def weight_grad(mixed, delta):
        cw = depth // shards
        parts = lax.dot_general(
            delta.reshape(count, n_node, n_fsdp, cw),
            mixed,
            (((0,), (0,)), ((), ())),
            preferred_element_type=jnp.float32,
        )
        parts = parts.transpose(1, 0, 2, 3).astype(jnp.bfloat16)
        inner = lax.all_to_all(parts, "fsdp", 0, 0, tiled=True)
        inner = jnp.sum(inner.astype(jnp.float32), axis=0).astype(jnp.bfloat16)
        outer = lax.all_to_all(inner, "node", 0, 0, tiled=True)
        summed = jnp.sum(outer.astype(jnp.float32), axis=0)
        return (summed / (groups * shards)).T

    mixed_one, first_matmul_result, whole_one = forward_layer(inputs, weight_one)
    latent_state = (
        jax.nn.silu(first_matmul_result).astype(jnp.bfloat16).reshape(groups, width, depth)
    )
    mixed_two, product_two, whole_two = forward_layer(latent_state, weight_two)
    delta_two = (
        final_layer_sensitivity.reshape(count, depth).astype(jnp.float32) * swish_slope(product_two)
    ).astype(jnp.bfloat16)
    grad_two = weight_grad(mixed_two, delta_two)
    upstream_second = back_weight(delta_two, weight_two)
    fetched_second = (normalizer_factor * upstream_second.reshape(groups, width, depth)).astype(
        jnp.bfloat16
    )
    delta_one = (
        spread_back(link, fetched_second).reshape(count, depth) * swish_slope(first_matmul_result)
    ).astype(jnp.bfloat16)
    grad_one = weight_grad(mixed_one, delta_one)
    upstream_first = back_weight(delta_one, weight_one)
    fetched_first = (normalizer_factor * upstream_first.reshape(groups, width, depth)).astype(
        jnp.bfloat16
    )
    input_grad = spread_back(link, fetched_first).astype(jnp.bfloat16).reshape(count, depth)
    source = jnp.full((shards, capacity), count, jnp.int32).at[owner, rank].set(
        jnp.arange(count, dtype=jnp.int32)
    )
    padded = jnp.concatenate([input_grad, jnp.zeros((1, depth), jnp.bfloat16)], axis=0)
    returned = exchange(padded[source])
    picks = (
        (safe_rows[..., None] == jnp.arange(rows_here, dtype=jnp.int32)) & valid[..., None]
    ).astype(jnp.bfloat16)
    table_grad = lax.dot_general(
        picks, returned, (((0, 1), (0, 1)), ((), ())), preferred_element_type=jnp.float32
    )
    return (table_grad, grad_one, grad_two)


def solution(mesh):
    placed = (
        P(AXES, None),
        P(AXES, None),
        P(AXES, None, None),
        P(None, "fsdp"),
        P(None, "fsdp"),
        P(AXES, None, None),
    )
    return jax.shard_map(
        on_device,
        mesh=mesh,
        in_specs=placed,
        out_specs=(P(AXES, None), P(None, AXES), P(None, AXES)),
        check_vma=False,
    )
```

```python
import jax
import jax.numpy as jnp
from jax import lax
from jax.sharding import PartitionSpec as P

AXES = ("node", "fsdp")


def swish_slope(values):
    sigma = jax.nn.sigmoid(values)
    return sigma * (1.0 + values * (1.0 - sigma))


def spread(link, values):
    return jnp.einsum("gij,gjd->gid", link, values, preferred_element_type=jnp.float32)


def spread_back(link, values):
    return jnp.einsum("gji,gjd->gid", link, values, preferred_element_type=jnp.float32)


def exchange(values):
    return lax.all_to_all(values, AXES, 0, 0, tiled=True)


def on_device(
    feature_table, vertex_labels, incidence_mask, weight_one, weight_two, final_layer_sensitivity
):
    groups, width = vertex_labels.shape
    count = groups * width
    n_node = lax.axis_size("node")
    n_fsdp = lax.axis_size("fsdp")
    shards = n_node * n_fsdp
    rows_here = feature_table.shape[0]
    depth = feature_table.shape[1]
    capacity = (2 * count + shards - 1) // shards + 1
    flat_ids = vertex_labels.reshape(count)
    owner = flat_ids // rows_here
    within = flat_ids % rows_here
    one_hot = (owner[:, None] == jnp.arange(shards, dtype=jnp.int32)[None, :]).astype(jnp.int32)
    before = jnp.cumsum(one_hot, axis=0) - one_hot
    rank = jnp.sum(before * one_hot, axis=1)
    position = owner * capacity + rank
    requests = jnp.full((shards * capacity,), -1, jnp.int32).at[position].set(within)
    asked = exchange(requests.reshape(shards, capacity))
    valid = asked >= 0
    safe_rows = jnp.maximum(asked, 0)
    picks = (
        (safe_rows[..., None] == jnp.arange(rows_here, dtype=jnp.int32)) & valid[..., None]
    ).astype(jnp.bfloat16)
    found = jnp.dot(picks, feature_table, preferred_element_type=jnp.float32).astype(jnp.bfloat16)
    answered = exchange(found)
    slot_of = (
        (owner[:, None, None] == jnp.arange(shards, dtype=jnp.int32)[:, None])
        & (rank[:, None, None] == jnp.arange(capacity, dtype=jnp.int32))
    ).astype(jnp.bfloat16)
    inputs = (
        lax.dot_general(
            slot_of, answered, (((1, 2), (0, 1)), ((), ())), preferred_element_type=jnp.float32
        )
        .astype(jnp.bfloat16)
        .reshape(groups, width, depth)
    )
    degree = jnp.sum(incidence_mask, axis=2).astype(jnp.float32)
    normalizer_factor = lax.rsqrt(1.0 + degree)[..., None]
    link = (incidence_mask + jnp.eye(width, dtype=jnp.int32)[None]).astype(jnp.bfloat16)

    def forward_layer(layer_in, weight):
        mixed = (
            (normalizer_factor * spread(link, layer_in)).astype(jnp.bfloat16).reshape(count, depth)
        )
        product = jnp.dot(
            mixed,
            lax.all_gather(weight, "fsdp", axis=1, tiled=True),
            preferred_element_type=jnp.float32,
        )
        return (mixed, product, weight)

    def back_weight(delta, weight):
        return lax.dot_general(
            delta,
            lax.all_gather(weight, "fsdp", axis=1, tiled=True),
            (((1,), (1,)), ((), ())),
            preferred_element_type=jnp.float32,
        )

    def weight_grad(mixed, delta):
        cw = depth // shards
        parts = lax.dot_general(
            delta.reshape(count, n_node, n_fsdp, cw),
            mixed,
            (((0,), (0,)), ((), ())),
            preferred_element_type=jnp.float32,
        )
        parts = parts.transpose(1, 0, 2, 3).astype(jnp.bfloat16)
        inner = lax.all_to_all(parts, "fsdp", 0, 0, tiled=True)
        inner = jnp.sum(inner.astype(jnp.float32), axis=0).astype(jnp.bfloat16)
        outer = lax.all_to_all(inner, "node", 0, 0, tiled=True)
        summed = jnp.sum(outer.astype(jnp.float32), axis=0)
        return (summed / (groups * shards)).T

    mixed_one, first_matmul_result, whole_one = forward_layer(inputs, weight_one)
    latent_state = (
        jax.nn.silu(first_matmul_result).astype(jnp.bfloat16).reshape(groups, width, depth)
    )
    mixed_two, product_two, whole_two = forward_layer(latent_state, weight_two)
    delta_two = (
        final_layer_sensitivity.reshape(count, depth).astype(jnp.float32) * swish_slope(product_two)
    ).astype(jnp.bfloat16)
    grad_two = weight_grad(mixed_two, delta_two)
    upstream_second = back_weight(delta_two, weight_two)
    fetched_second = (normalizer_factor * upstream_second.reshape(groups, width, depth)).astype(
        jnp.bfloat16
    )
    delta_one = (
        spread_back(link, fetched_second).reshape(count, depth) * swish_slope(first_matmul_result)
    ).astype(jnp.bfloat16)
    grad_one = weight_grad(mixed_one, delta_one)
    upstream_first = back_weight(delta_one, weight_one)
    fetched_first = (normalizer_factor * upstream_first.reshape(groups, width, depth)).astype(
        jnp.bfloat16
    )
    input_grad = spread_back(link, fetched_first).astype(jnp.bfloat16).reshape(count, depth)
    outgoing = lax.dot_general(
        slot_of, input_grad, (((0,), (0,)), ((), ())), preferred_element_type=jnp.float32
    ).astype(jnp.bfloat16)
    returned = exchange(outgoing)
    table_grad = lax.dot_general(
        picks, returned, (((0, 1), (0, 1)), ((), ())), preferred_element_type=jnp.float32
    )
    return (table_grad, grad_one, grad_two)


def solution(mesh):
    placed = (
        P(AXES, None),
        P(AXES, None),
        P(AXES, None, None),
        P(None, "fsdp"),
        P(None, "fsdp"),
        P(AXES, None, None),
    )
    return jax.shard_map(
        on_device,
        mesh=mesh,
        in_specs=placed,
        out_specs=(P(AXES, None), P(None, AXES), P(None, AXES)),
        check_vma=False,
    )
```

```python
import jax
import jax.numpy as jnp
from jax import lax
from jax.sharding import PartitionSpec as P

AXES = ("node", "fsdp")


def swish_slope(values):
    sigma = jax.nn.sigmoid(values)
    return sigma * (1.0 + values * (1.0 - sigma))


def spread(link, values):
    return jnp.einsum("gij,gjd->gid", link, values, preferred_element_type=jnp.float32)


def spread_back(link, values):
    return jnp.einsum("gji,gjd->gid", link, values, preferred_element_type=jnp.float32)


def exchange(values):
    return lax.all_to_all(values, AXES, 0, 0, tiled=True)


def on_device(
    feature_table, vertex_labels, incidence_mask, weight_one, weight_two, final_layer_sensitivity
):
    groups, width = vertex_labels.shape
    count = groups * width
    n_node = lax.axis_size("node")
    n_fsdp = lax.axis_size("fsdp")
    shards = n_node * n_fsdp
    rows_here = feature_table.shape[0]
    depth = feature_table.shape[1]
    capacity = (2 * count + shards - 1) // shards + 1
    flat_ids = vertex_labels.reshape(count)
    owner = flat_ids // rows_here
    within = flat_ids % rows_here
    one_hot = (owner[:, None] == jnp.arange(shards, dtype=jnp.int32)[None, :]).astype(jnp.int32)
    before = jnp.cumsum(one_hot, axis=0) - one_hot
    rank = jnp.sum(before * one_hot, axis=1)
    position = owner * capacity + rank
    requests = jnp.full((shards * capacity,), -1, jnp.int32).at[position].set(within)
    asked = exchange(requests.reshape(shards, capacity))
    valid = asked >= 0
    safe_rows = jnp.maximum(asked, 0)
    picks = (
        (safe_rows[..., None] == jnp.arange(rows_here, dtype=jnp.int32)) & valid[..., None]
    ).astype(jnp.bfloat16)
    found = jnp.dot(picks, feature_table, preferred_element_type=jnp.float32).astype(jnp.bfloat16)
    answered = exchange(found)
    slot_of = (
        (owner[:, None, None] == jnp.arange(shards, dtype=jnp.int32)[:, None])
        & (rank[:, None, None] == jnp.arange(capacity, dtype=jnp.int32))
    ).astype(jnp.bfloat16)
    inputs = (
        lax.dot_general(
            slot_of, answered, (((1, 2), (0, 1)), ((), ())), preferred_element_type=jnp.float32
        )
        .astype(jnp.bfloat16)
        .reshape(groups, width, depth)
    )
    degree = jnp.sum(incidence_mask, axis=2).astype(jnp.float32)
    normalizer_factor = lax.rsqrt(1.0 + degree)[..., None]
    link = (incidence_mask + jnp.eye(width, dtype=jnp.int32)[None]).astype(jnp.bfloat16)

    def forward_layer(layer_in, weight):
        mixed = (
            (normalizer_factor * spread(link, layer_in)).astype(jnp.bfloat16).reshape(count, depth)
        )
        product = jnp.dot(
            mixed,
            lax.all_gather(weight, "fsdp", axis=1, tiled=True),
            preferred_element_type=jnp.float32,
        )
        return (mixed, product, weight)

    def back_weight(delta, weight):
        return lax.dot_general(
            delta,
            lax.all_gather(weight, "fsdp", axis=1, tiled=True),
            (((1,), (1,)), ((), ())),
            preferred_element_type=jnp.float32,
        )

    def weight_grad(mixed, delta):
        cw = depth // shards
        parts = lax.dot_general(
            delta.reshape(count, n_node, n_fsdp, cw),
            mixed,
            (((0,), (0,)), ((), ())),
            preferred_element_type=jnp.float32,
        )
        parts = parts.transpose(1, 0, 2, 3).astype(jnp.bfloat16)
        inner = lax.all_to_all(parts, "fsdp", 0, 0, tiled=True)
        inner = jnp.sum(inner.astype(jnp.float32), axis=0)
        summed = lax.psum_scatter(inner, "node", scatter_dimension=0, tiled=True)
        return (summed.reshape(cw, depth) / (groups * shards)).T

    mixed_one, first_matmul_result, whole_one = forward_layer(inputs, weight_one)
    latent_state = (
        jax.nn.silu(first_matmul_result).astype(jnp.bfloat16).reshape(groups, width, depth)
    )
    mixed_two, product_two, whole_two = forward_layer(latent_state, weight_two)
    delta_two = (
        final_layer_sensitivity.reshape(count, depth).astype(jnp.float32) * swish_slope(product_two)
    ).astype(jnp.bfloat16)
    grad_two = weight_grad(mixed_two, delta_two)
    upstream_second = back_weight(delta_two, weight_two)
    fetched_second = (normalizer_factor * upstream_second.reshape(groups, width, depth)).astype(
        jnp.bfloat16
    )
    delta_one = (
        spread_back(link, fetched_second).reshape(count, depth) * swish_slope(first_matmul_result)
    ).astype(jnp.bfloat16)
    grad_one = weight_grad(mixed_one, delta_one)
    upstream_first = back_weight(delta_one, weight_one)
    fetched_first = (normalizer_factor * upstream_first.reshape(groups, width, depth)).astype(
        jnp.bfloat16
    )
    input_grad = spread_back(link, fetched_first).astype(jnp.bfloat16).reshape(count, depth)
    outgoing = lax.dot_general(
        slot_of, input_grad, (((0,), (0,)), ((), ())), preferred_element_type=jnp.float32
    ).astype(jnp.bfloat16)
    returned = exchange(outgoing)
    table_grad = lax.dot_general(
        picks, returned, (((0, 1), (0, 1)), ((), ())), preferred_element_type=jnp.float32
    )
    return (table_grad, grad_one, grad_two)


def solution(mesh):
    placed = (
        P(AXES, None),
        P(AXES, None),
        P(AXES, None, None),
        P(None, "fsdp"),
        P(None, "fsdp"),
        P(AXES, None, None),
    )
    return jax.shard_map(
        on_device,
        mesh=mesh,
        in_specs=placed,
        out_specs=(P(AXES, None), P(None, AXES), P(None, AXES)),
        check_vma=False,
    )
```

```python
import jax
import jax.numpy as jnp
from jax import lax
from jax.sharding import PartitionSpec as P

AXES = ("node", "fsdp")


def swish_slope(values):
    sigma = jax.nn.sigmoid(values)
    return sigma * (1.0 + values * (1.0 - sigma))


def spread(link, values):
    return jnp.einsum("gij,gjd->gid", link, values, preferred_element_type=jnp.float32)


def spread_back(link, values):
    return jnp.einsum("gji,gjd->gid", link, values, preferred_element_type=jnp.float32)


def exchange(values):
    return lax.all_to_all(values, AXES, 0, 0, tiled=True)


def on_device(
    feature_table, vertex_labels, incidence_mask, weight_one, weight_two, final_layer_sensitivity
):
    groups, width = vertex_labels.shape
    count = groups * width
    n_node = lax.axis_size("node")
    n_fsdp = lax.axis_size("fsdp")
    shards = n_node * n_fsdp
    rows_here = feature_table.shape[0]
    depth = feature_table.shape[1]
    capacity = (2 * count + shards - 1) // shards + 1
    flat_ids = vertex_labels.reshape(count)
    owner = flat_ids // rows_here
    within = flat_ids % rows_here
    one_hot = (owner[:, None] == jnp.arange(shards, dtype=jnp.int32)[None, :]).astype(jnp.int32)
    before = jnp.cumsum(one_hot, axis=0) - one_hot
    rank = jnp.sum(before * one_hot, axis=1)
    position = owner * capacity + rank
    requests = jnp.full((shards * capacity,), -1, jnp.int32).at[position].set(within)
    asked = exchange(requests.reshape(shards, capacity))
    valid = asked >= 0
    safe_rows = jnp.maximum(asked, 0)
    picks = (
        (safe_rows[..., None] == jnp.arange(rows_here, dtype=jnp.int32)) & valid[..., None]
    ).astype(jnp.bfloat16)
    found = jnp.dot(picks, feature_table, preferred_element_type=jnp.float32).astype(jnp.bfloat16)
    answered = exchange(found)
    slot_of = (
        (owner[:, None, None] == jnp.arange(shards, dtype=jnp.int32)[:, None])
        & (rank[:, None, None] == jnp.arange(capacity, dtype=jnp.int32))
    ).astype(jnp.bfloat16)
    inputs = (
        lax.dot_general(
            slot_of, answered, (((1, 2), (0, 1)), ((), ())), preferred_element_type=jnp.float32
        )
        .astype(jnp.bfloat16)
        .reshape(groups, width, depth)
    )
    degree = jnp.sum(incidence_mask, axis=2).astype(jnp.float32)
    normalizer_factor = lax.rsqrt(1.0 + degree)[..., None]
    link = (incidence_mask + jnp.eye(width, dtype=jnp.int32)[None]).astype(jnp.bfloat16)

    def forward_layer(layer_in, weight):
        mixed = (
            (normalizer_factor * spread(link, layer_in)).astype(jnp.bfloat16).reshape(count, depth)
        )
        product = jnp.dot(
            mixed,
            lax.all_gather(weight, "fsdp", axis=1, tiled=True),
            preferred_element_type=jnp.float32,
        )
        return (mixed, product, weight)

    def back_weight(delta, weight):
        return lax.dot_general(
            delta,
            lax.all_gather(weight, "fsdp", axis=1, tiled=True),
            (((1,), (1,)), ((), ())),
            preferred_element_type=jnp.float32,
        )

    def grad_parts(mixed, delta):
        return lax.dot_general(
            delta.reshape(count, shards, depth // shards),
            mixed,
            (((0,), (0,)), ((), ())),
            preferred_element_type=jnp.float32,
        )

    def reduce_blocks(parts):
        me = lax.axis_index(AXES)
        step = 1
        while step < shards:
            held = parts.shape[1]
            pair = parts.reshape(parts.shape[0], held // 2, 2, *parts.shape[2:])
            upper = (me // step) % 2 == 1
            keep = jnp.where(upper, pair[:, :, 1], pair[:, :, 0])
            send = jnp.where(upper, pair[:, :, 0], pair[:, :, 1])
            if step > 1:
                send = send.astype(jnp.bfloat16)
            moved = lax.ppermute(send, AXES, [(i, i ^ step) for i in range(shards)])
            parts = keep + moved.astype(jnp.float32)
            step *= 2
        return parts[:, 0] / (groups * shards)

    mixed_one, first_matmul_result, whole_one = forward_layer(inputs, weight_one)
    latent_state = (
        jax.nn.silu(first_matmul_result).astype(jnp.bfloat16).reshape(groups, width, depth)
    )
    mixed_two, product_two, whole_two = forward_layer(latent_state, weight_two)
    delta_two = (
        final_layer_sensitivity.reshape(count, depth).astype(jnp.float32) * swish_slope(product_two)
    ).astype(jnp.bfloat16)
    parts_two = grad_parts(mixed_two, delta_two)
    upstream_second = back_weight(delta_two, weight_two)
    fetched_second = (normalizer_factor * upstream_second.reshape(groups, width, depth)).astype(
        jnp.bfloat16
    )
    delta_one = (
        spread_back(link, fetched_second).reshape(count, depth) * swish_slope(first_matmul_result)
    ).astype(jnp.bfloat16)
    parts_one = grad_parts(mixed_one, delta_one)
    upstream_first = back_weight(delta_one, weight_one)
    fetched_first = (normalizer_factor * upstream_first.reshape(groups, width, depth)).astype(
        jnp.bfloat16
    )
    input_grad = spread_back(link, fetched_first).astype(jnp.bfloat16).reshape(count, depth)
    outgoing = lax.dot_general(
        slot_of, input_grad, (((0,), (0,)), ((), ())), preferred_element_type=jnp.float32
    ).astype(jnp.bfloat16)
    returned = exchange(outgoing)
    table_grad = lax.dot_general(
        picks, returned, (((0, 1), (0, 1)), ((), ())), preferred_element_type=jnp.float32
    )
    grads = reduce_blocks(jnp.stack([parts_one, parts_two]))
    return (table_grad, grads[0].T, grads[1].T)


def solution(mesh):
    placed = (
        P(AXES, None),
        P(AXES, None),
        P(AXES, None, None),
        P(None, "fsdp"),
        P(None, "fsdp"),
        P(AXES, None, None),
    )
    return jax.shard_map(
        on_device,
        mesh=mesh,
        in_specs=placed,
        out_specs=(P(AXES, None), P(None, AXES), P(None, AXES)),
        check_vma=False,
    )
```

```python
import jax
import jax.numpy as jnp
from jax import lax
from jax.sharding import PartitionSpec as P

AXES = ("node", "fsdp")


def swish_slope(values):
    sigma = jax.nn.sigmoid(values)
    return sigma * (1.0 + values * (1.0 - sigma))


def spread(link, values):
    return jnp.einsum("gij,gjd->gid", link, values, preferred_element_type=jnp.float32)


def spread_back(link, values):
    return jnp.einsum("gji,gjd->gid", link, values, preferred_element_type=jnp.float32)


def exchange(values):
    return lax.all_to_all(values, AXES, 0, 0, tiled=True)


def on_device(
    feature_table, vertex_labels, incidence_mask, weight_one, weight_two, final_layer_sensitivity
):
    groups, width = vertex_labels.shape
    count = groups * width
    n_node = lax.axis_size("node")
    n_fsdp = lax.axis_size("fsdp")
    shards = n_node * n_fsdp
    rows_here = feature_table.shape[0]
    depth = feature_table.shape[1]
    capacity = (2 * count + shards - 1) // shards + 1
    flat_ids = vertex_labels.reshape(count)
    owner = flat_ids // rows_here
    within = flat_ids % rows_here
    one_hot = (owner[:, None] == jnp.arange(shards, dtype=jnp.int32)[None, :]).astype(jnp.int32)
    before = jnp.cumsum(one_hot, axis=0) - one_hot
    rank = jnp.sum(before * one_hot, axis=1)
    position = owner * capacity + rank
    requests = jnp.full((shards * capacity,), -1, jnp.int32).at[position].set(within)
    asked = exchange(requests.reshape(shards, capacity))
    valid = asked >= 0
    safe_rows = jnp.maximum(asked, 0)
    picks = (
        (safe_rows[..., None] == jnp.arange(rows_here, dtype=jnp.int32)) & valid[..., None]
    ).astype(jnp.bfloat16)
    found = jnp.dot(picks, feature_table, preferred_element_type=jnp.float32).astype(jnp.bfloat16)
    answered = exchange(found)
    slot_of = (
        (owner[:, None, None] == jnp.arange(shards, dtype=jnp.int32)[:, None])
        & (rank[:, None, None] == jnp.arange(capacity, dtype=jnp.int32))
    ).astype(jnp.bfloat16)
    inputs = (
        lax.dot_general(
            slot_of, answered, (((1, 2), (0, 1)), ((), ())), preferred_element_type=jnp.float32
        )
        .astype(jnp.bfloat16)
        .reshape(groups, width, depth)
    )
    degree = jnp.sum(incidence_mask, axis=2).astype(jnp.float32)
    normalizer_factor = lax.rsqrt(1.0 + degree)[..., None]
    link = (incidence_mask + jnp.eye(width, dtype=jnp.int32)[None]).astype(jnp.bfloat16)

    def forward_layer(layer_in, weight):
        mixed = (
            (normalizer_factor * spread(link, layer_in)).astype(jnp.bfloat16).reshape(count, depth)
        )
        product = jnp.dot(
            mixed,
            lax.all_gather(weight, "fsdp", axis=1, tiled=True),
            preferred_element_type=jnp.float32,
        )
        return (mixed, product, weight)

    def back_weight(delta, weight):
        return lax.dot_general(
            delta,
            lax.all_gather(weight, "fsdp", axis=1, tiled=True),
            (((1,), (1,)), ((), ())),
            preferred_element_type=jnp.float32,
        )

    def grad_parts(mixed, delta):
        return lax.dot_general(
            delta.reshape(count, shards, depth // shards),
            mixed,
            (((0,), (0,)), ((), ())),
            preferred_element_type=jnp.float32,
        )

    def reduce_blocks(parts):
        me = lax.axis_index(AXES)
        step = 1
        while step < shards:
            held = parts.shape[1]
            pair = parts.reshape(parts.shape[0], held // 2, 2, *parts.shape[2:])
            upper = (me // step) % 2 == 1
            keep = jnp.where(upper, pair[:, :, 1], pair[:, :, 0])
            send = jnp.where(upper, pair[:, :, 0], pair[:, :, 1])
            if step > 1:
                send = send.astype(jnp.bfloat16)
            moved = lax.ppermute(send, AXES, [(i, i ^ step) for i in range(shards)])
            parts = keep + moved.astype(jnp.float32)
            step *= 2
        return parts[:, 0] / (groups * shards)

    mixed_one, first_matmul_result, whole_one = forward_layer(inputs, weight_one)
    latent_state = (
        jax.nn.silu(first_matmul_result).astype(jnp.bfloat16).reshape(groups, width, depth)
    )
    mixed_two, product_two, whole_two = forward_layer(latent_state, weight_two)
    delta_two = (
        final_layer_sensitivity.reshape(count, depth).astype(jnp.float32) * swish_slope(product_two)
    ).astype(jnp.bfloat16)
    parts_two = grad_parts(mixed_two, delta_two)
    upstream_second = back_weight(delta_two, weight_two)
    fetched_second = (normalizer_factor * upstream_second.reshape(groups, width, depth)).astype(
        jnp.bfloat16
    )
    delta_one = (
        spread_back(link, fetched_second).reshape(count, depth) * swish_slope(first_matmul_result)
    ).astype(jnp.bfloat16)
    parts_one = grad_parts(mixed_one, delta_one)
    upstream_first = back_weight(delta_one, weight_one)
    fetched_first = (normalizer_factor * upstream_first.reshape(groups, width, depth)).astype(
        jnp.bfloat16
    )
    input_grad = spread_back(link, fetched_first).astype(jnp.bfloat16).reshape(count, depth)
    outgoing = lax.dot_general(
        slot_of, input_grad, (((0,), (0,)), ((), ())), preferred_element_type=jnp.float32
    ).astype(jnp.bfloat16)
    returned = exchange(outgoing)
    table_grad = lax.dot_general(
        picks, returned, (((0, 1), (0, 1)), ((), ())), preferred_element_type=jnp.float32
    )
    grad_one = reduce_blocks(parts_one[None])[0].T
    grad_two = reduce_blocks(parts_two[None])[0].T
    return (table_grad, grad_one, grad_two)


def solution(mesh):
    placed = (
        P(AXES, None),
        P(AXES, None),
        P(AXES, None, None),
        P(None, "fsdp"),
        P(None, "fsdp"),
        P(AXES, None, None),
    )
    return jax.shard_map(
        on_device,
        mesh=mesh,
        in_specs=placed,
        out_specs=(P(AXES, None), P(None, AXES), P(None, AXES)),
        check_vma=False,
    )
```

```python
import jax
import jax.numpy as jnp
from jax import lax
from jax.sharding import PartitionSpec as P

AXES = ("node", "fsdp")


def swish_slope(values):
    sigma = jax.nn.sigmoid(values)
    return sigma * (1.0 + values * (1.0 - sigma))


def spread(link, values):
    return jnp.einsum("gij,gjd->gid", link, values, preferred_element_type=jnp.float32)


def spread_back(link, values):
    return jnp.einsum("gji,gjd->gid", link, values, preferred_element_type=jnp.float32)


def exchange(values):
    return lax.all_to_all(values, AXES, 0, 0, tiled=True)


def on_device(
    feature_table, vertex_labels, incidence_mask, weight_one, weight_two, final_layer_sensitivity
):
    groups, width = vertex_labels.shape
    count = groups * width
    n_node = lax.axis_size("node")
    n_fsdp = lax.axis_size("fsdp")
    shards = n_node * n_fsdp
    rows_here = feature_table.shape[0]
    depth = feature_table.shape[1]
    capacity = (2 * count + shards - 1) // shards + 1
    flat_ids = vertex_labels.reshape(count)
    owner = flat_ids // rows_here
    within = flat_ids % rows_here
    one_hot = (owner[:, None] == jnp.arange(shards, dtype=jnp.int32)[None, :]).astype(jnp.int32)
    before = jnp.cumsum(one_hot, axis=0) - one_hot
    rank = jnp.sum(before * one_hot, axis=1)
    position = owner * capacity + rank
    requests = jnp.full((shards * capacity,), -1, jnp.int32).at[position].set(within)
    asked = exchange(requests.reshape(shards, capacity))
    valid = asked >= 0
    safe_rows = jnp.maximum(asked, 0)
    picks = (
        (safe_rows[..., None] == jnp.arange(rows_here, dtype=jnp.int32)) & valid[..., None]
    ).astype(jnp.bfloat16)
    found = jnp.dot(picks, feature_table, preferred_element_type=jnp.float32).astype(jnp.bfloat16)
    answered = exchange(found)
    slot_of = (
        (owner[:, None, None] == jnp.arange(shards, dtype=jnp.int32)[:, None])
        & (rank[:, None, None] == jnp.arange(capacity, dtype=jnp.int32))
    ).astype(jnp.bfloat16)
    inputs = (
        lax.dot_general(
            slot_of, answered, (((1, 2), (0, 1)), ((), ())), preferred_element_type=jnp.float32
        )
        .astype(jnp.bfloat16)
        .reshape(groups, width, depth)
    )
    degree = jnp.sum(incidence_mask, axis=2).astype(jnp.float32)
    normalizer_factor = lax.rsqrt(1.0 + degree)[..., None]
    link = (incidence_mask + jnp.eye(width, dtype=jnp.int32)[None]).astype(jnp.bfloat16)

    def forward_layer(layer_in, weight):
        mixed = (
            (normalizer_factor * spread(link, layer_in)).astype(jnp.bfloat16).reshape(count, depth)
        )
        product = jnp.dot(
            mixed,
            lax.all_gather(weight, "fsdp", axis=1, tiled=True),
            preferred_element_type=jnp.float32,
        )
        return (mixed, product, weight)

    def back_weight(delta, weight):
        return lax.dot_general(
            delta,
            lax.all_gather(weight, "fsdp", axis=1, tiled=True),
            (((1,), (1,)), ((), ())),
            preferred_element_type=jnp.float32,
        )

    def grad_parts(mixed, delta):
        return lax.dot_general(
            delta.reshape(count, shards, depth // shards),
            mixed,
            (((0,), (0,)), ((), ())),
            preferred_element_type=jnp.float32,
        )

    def reduce_blocks(parts, step, stop):
        me = lax.axis_index(AXES)
        while step < stop:
            held = parts.shape[1]
            pair = parts.reshape(parts.shape[0], held // 2, 2, *parts.shape[2:])
            upper = (me // step) % 2 == 1
            keep = jnp.where(upper, pair[:, :, 1], pair[:, :, 0])
            send = jnp.where(upper, pair[:, :, 0], pair[:, :, 1])
            if step > 1:
                send = send.astype(jnp.bfloat16)
            moved = lax.ppermute(send, AXES, [(i, i ^ step) for i in range(shards)])
            parts = keep + moved.astype(jnp.float32)
            step *= 2
        return parts

    def finish(parts):
        return (parts[0, 0] / (groups * shards)).T

    mixed_one, first_matmul_result, whole_one = forward_layer(inputs, weight_one)
    latent_state = (
        jax.nn.silu(first_matmul_result).astype(jnp.bfloat16).reshape(groups, width, depth)
    )
    mixed_two, product_two, whole_two = forward_layer(latent_state, weight_two)
    delta_two = (
        final_layer_sensitivity.reshape(count, depth).astype(jnp.float32) * swish_slope(product_two)
    ).astype(jnp.bfloat16)
    parts_two = grad_parts(mixed_two, delta_two)
    upstream_second = back_weight(delta_two, weight_two)
    fetched_second = (normalizer_factor * upstream_second.reshape(groups, width, depth)).astype(
        jnp.bfloat16
    )
    delta_one = (
        spread_back(link, fetched_second).reshape(count, depth) * swish_slope(first_matmul_result)
    ).astype(jnp.bfloat16)
    parts_one = grad_parts(mixed_one, delta_one)
    upstream_first = back_weight(delta_one, weight_one)
    fetched_first = (normalizer_factor * upstream_first.reshape(groups, width, depth)).astype(
        jnp.bfloat16
    )
    input_grad = spread_back(link, fetched_first).astype(jnp.bfloat16).reshape(count, depth)
    outgoing = lax.dot_general(
        slot_of, input_grad, (((0,), (0,)), ((), ())), preferred_element_type=jnp.float32
    ).astype(jnp.bfloat16)
    early = min(4, shards)
    parts_two = reduce_blocks(parts_two[None], 1, early)
    outgoing, parts_two = lax.optimization_barrier((outgoing, parts_two))
    returned = exchange(outgoing)
    table_grad = lax.dot_general(
        picks, returned, (((0, 1), (0, 1)), ((), ())), preferred_element_type=jnp.float32
    )
    grad_one = finish(reduce_blocks(parts_one[None], 1, shards))
    grad_two = finish(reduce_blocks(parts_two, early, shards))
    return (table_grad, grad_one, grad_two)


def solution(mesh):
    placed = (
        P(AXES, None),
        P(AXES, None),
        P(AXES, None, None),
        P(None, "fsdp"),
        P(None, "fsdp"),
        P(AXES, None, None),
    )
    return jax.shard_map(
        on_device,
        mesh=mesh,
        in_specs=placed,
        out_specs=(P(AXES, None), P(None, AXES), P(None, AXES)),
        check_vma=False,
    )
```

```python
import jax
import jax.numpy as jnp
from jax import lax
from jax.sharding import PartitionSpec as P

AXES = ("node", "fsdp")


def swish_slope(values):
    sigma = jax.nn.sigmoid(values)
    return sigma * (1.0 + values * (1.0 - sigma))


def spread(link, values):
    return jnp.einsum("gij,gjd->gid", link, values, preferred_element_type=jnp.float32)


def spread_back(link, values):
    return jnp.einsum("gji,gjd->gid", link, values, preferred_element_type=jnp.float32)


def exchange(values):
    return lax.all_to_all(values, AXES, 0, 0, tiled=True)


def on_device(
    feature_table, vertex_labels, incidence_mask, weight_one, weight_two, final_layer_sensitivity
):
    groups, width = vertex_labels.shape
    count = groups * width
    n_node = lax.axis_size("node")
    n_fsdp = lax.axis_size("fsdp")
    shards = n_node * n_fsdp
    rows_here = feature_table.shape[0]
    depth = feature_table.shape[1]
    capacity = (2 * count + shards - 1) // shards + 1
    flat_ids = vertex_labels.reshape(count)
    owner = flat_ids // rows_here
    within = flat_ids % rows_here
    one_hot = (owner[:, None] == jnp.arange(shards, dtype=jnp.int32)[None, :]).astype(jnp.int32)
    before = jnp.cumsum(one_hot, axis=0) - one_hot
    rank = jnp.sum(before * one_hot, axis=1)
    position = owner * capacity + rank
    requests = jnp.full((shards * capacity,), -1, jnp.int32).at[position].set(within)
    asked = exchange(requests.reshape(shards, capacity))
    valid = asked >= 0
    safe_rows = jnp.maximum(asked, 0)
    picks = (
        (safe_rows[..., None] == jnp.arange(rows_here, dtype=jnp.int32)) & valid[..., None]
    ).astype(jnp.bfloat16)
    found = jnp.dot(picks, feature_table, preferred_element_type=jnp.float32).astype(jnp.bfloat16)
    answered = exchange(found)
    slot_of = (
        (owner[:, None, None] == jnp.arange(shards, dtype=jnp.int32)[:, None])
        & (rank[:, None, None] == jnp.arange(capacity, dtype=jnp.int32))
    ).astype(jnp.bfloat16)
    degree = jnp.sum(incidence_mask, axis=2).astype(jnp.float32)
    normalizer_factor = lax.rsqrt(1.0 + degree)[..., None]
    link = (incidence_mask + jnp.eye(width, dtype=jnp.int32)[None]).astype(jnp.bfloat16)
    linked_slots = (
        jnp.einsum(
            "gij,gjsc->gisc",
            link,
            slot_of.reshape(groups, width, shards, capacity),
            preferred_element_type=jnp.float32,
        )
        .astype(jnp.bfloat16)
        .reshape(count, shards, capacity)
    )
    spread_in = lax.dot_general(
        linked_slots, answered, (((1, 2), (0, 1)), ((), ())), preferred_element_type=jnp.float32
    )

    def forward_layer(layer_in, weight, spread_done=None):
        if spread_done is None:
            spread_done = spread(link, layer_in)
        mixed = (
            (normalizer_factor * spread_done.reshape(groups, width, depth))
            .astype(jnp.bfloat16)
            .reshape(count, depth)
        )
        product = jnp.dot(
            mixed,
            lax.all_gather(weight, "fsdp", axis=1, tiled=True),
            preferred_element_type=jnp.float32,
        )
        return (mixed, product, weight)

    def back_weight(delta, weight):
        return lax.dot_general(
            delta,
            lax.all_gather(weight, "fsdp", axis=1, tiled=True),
            (((1,), (1,)), ((), ())),
            preferred_element_type=jnp.float32,
        )

    def grad_parts(mixed, delta):
        return lax.dot_general(
            delta.reshape(count, shards, depth // shards),
            mixed,
            (((0,), (0,)), ((), ())),
            preferred_element_type=jnp.float32,
        )

    def reduce_blocks(parts):
        me = lax.axis_index(AXES)
        step = 1
        while step < shards:
            held = parts.shape[1]
            pair = parts.reshape(parts.shape[0], held // 2, 2, *parts.shape[2:])
            upper = (me // step) % 2 == 1
            keep = jnp.where(upper, pair[:, :, 1], pair[:, :, 0])
            send = jnp.where(upper, pair[:, :, 0], pair[:, :, 1])
            if step > 1:
                send = send.astype(jnp.bfloat16)
            moved = lax.ppermute(send, AXES, [(i, i ^ step) for i in range(shards)])
            parts = keep + moved.astype(jnp.float32)
            step *= 2
        return parts[:, 0] / (groups * shards)

    mixed_one, first_matmul_result, whole_one = forward_layer(None, weight_one, spread_in)
    latent_state = (
        jax.nn.silu(first_matmul_result).astype(jnp.bfloat16).reshape(groups, width, depth)
    )
    mixed_two, product_two, whole_two = forward_layer(latent_state, weight_two)
    delta_two = (
        final_layer_sensitivity.reshape(count, depth).astype(jnp.float32) * swish_slope(product_two)
    ).astype(jnp.bfloat16)
    parts_two = grad_parts(mixed_two, delta_two)
    upstream_second = back_weight(delta_two, weight_two)
    fetched_second = (normalizer_factor * upstream_second.reshape(groups, width, depth)).astype(
        jnp.bfloat16
    )
    delta_one = (
        spread_back(link, fetched_second).reshape(count, depth) * swish_slope(first_matmul_result)
    ).astype(jnp.bfloat16)
    parts_one = grad_parts(mixed_one, delta_one)
    upstream_first = back_weight(delta_one, weight_one)
    fetched_first = (normalizer_factor * upstream_first.reshape(groups, width, depth)).astype(
        jnp.bfloat16
    )
    outgoing = lax.dot_general(
        linked_slots,
        fetched_first.reshape(count, depth),
        (((0,), (0,)), ((), ())),
        preferred_element_type=jnp.float32,
    ).astype(jnp.bfloat16)
    returned = exchange(outgoing)
    table_grad = lax.dot_general(
        picks, returned, (((0, 1), (0, 1)), ((), ())), preferred_element_type=jnp.float32
    )
    grad_one = reduce_blocks(parts_one[None])[0].T
    grad_two = reduce_blocks(parts_two[None])[0].T
    return (table_grad, grad_one, grad_two)


def solution(mesh):
    placed = (
        P(AXES, None),
        P(AXES, None),
        P(AXES, None, None),
        P(None, "fsdp"),
        P(None, "fsdp"),
        P(AXES, None, None),
    )
    return jax.shard_map(
        on_device,
        mesh=mesh,
        in_specs=placed,
        out_specs=(P(AXES, None), P(None, AXES), P(None, AXES)),
        check_vma=False,
    )
```

```python
import jax
import jax.numpy as jnp
from jax import lax
from jax.sharding import PartitionSpec as P

AXES = ("node", "fsdp")


def swish_slope(values):
    sigma = jax.nn.sigmoid(values)
    return sigma * (1.0 + values * (1.0 - sigma))


def spread(link, values):
    return jnp.einsum("gij,gjd->gid", link, values, preferred_element_type=jnp.float32)


def spread_back(link, values):
    return jnp.einsum("gji,gjd->gid", link, values, preferred_element_type=jnp.float32)


def exchange(values):
    return lax.all_to_all(values, AXES, 0, 0, tiled=True)


def on_device(
    feature_table, vertex_labels, incidence_mask, weight_one, weight_two, final_layer_sensitivity
):
    groups, width = vertex_labels.shape
    count = groups * width
    n_node = lax.axis_size("node")
    n_fsdp = lax.axis_size("fsdp")
    shards = n_node * n_fsdp
    rows_here = feature_table.shape[0]
    depth = feature_table.shape[1]
    capacity = (2 * count + shards - 1) // shards + 1
    flat_ids = vertex_labels.reshape(count)
    owner = flat_ids // rows_here
    within = flat_ids % rows_here
    one_hot = (owner[:, None] == jnp.arange(shards, dtype=jnp.int32)[None, :]).astype(jnp.int32)
    before = jnp.cumsum(one_hot, axis=0) - one_hot
    rank = jnp.sum(before * one_hot, axis=1)
    every_id = lax.all_gather(flat_ids, AXES)
    mine = (every_id // rows_here == lax.axis_index(AXES)).astype(jnp.int32)
    order = jnp.cumsum(mine, axis=1) - mine
    hit = (mine[..., None] > 0) & (order[..., None] == jnp.arange(capacity, dtype=jnp.int32))
    asked = jnp.sum(jnp.where(hit, (every_id % rows_here + 1)[..., None], 0), axis=1) - 1
    valid = asked >= 0
    safe_rows = jnp.maximum(asked, 0)
    picks = (
        (safe_rows[..., None] == jnp.arange(rows_here, dtype=jnp.int32)) & valid[..., None]
    ).astype(jnp.bfloat16)
    found = jnp.dot(picks, feature_table, preferred_element_type=jnp.float32).astype(jnp.bfloat16)
    answered = exchange(found)
    slot_of = (
        (owner[:, None, None] == jnp.arange(shards, dtype=jnp.int32)[:, None])
        & (rank[:, None, None] == jnp.arange(capacity, dtype=jnp.int32))
    ).astype(jnp.bfloat16)
    degree = jnp.sum(incidence_mask, axis=2).astype(jnp.float32)
    normalizer_factor = lax.rsqrt(1.0 + degree)[..., None]
    link = (incidence_mask + jnp.eye(width, dtype=jnp.int32)[None]).astype(jnp.bfloat16)
    linked_slots = (
        jnp.einsum(
            "gij,gjsc->gisc",
            link,
            slot_of.reshape(groups, width, shards, capacity),
            preferred_element_type=jnp.float32,
        )
        .astype(jnp.bfloat16)
        .reshape(count, shards, capacity)
    )
    spread_in = lax.dot_general(
        linked_slots, answered, (((1, 2), (0, 1)), ((), ())), preferred_element_type=jnp.float32
    )

    def forward_layer(layer_in, weight, spread_done=None):
        if spread_done is None:
            spread_done = spread(link, layer_in)
        mixed = (
            (normalizer_factor * spread_done.reshape(groups, width, depth))
            .astype(jnp.bfloat16)
            .reshape(count, depth)
        )
        product = jnp.dot(
            mixed,
            lax.all_gather(weight, "fsdp", axis=1, tiled=True),
            preferred_element_type=jnp.float32,
        )
        return (mixed, product, weight)

    def back_weight(delta, weight):
        return lax.dot_general(
            delta,
            lax.all_gather(weight, "fsdp", axis=1, tiled=True),
            (((1,), (1,)), ((), ())),
            preferred_element_type=jnp.float32,
        )

    def grad_parts(mixed, delta):
        return lax.dot_general(
            delta.reshape(count, shards, depth // shards),
            mixed,
            (((0,), (0,)), ((), ())),
            preferred_element_type=jnp.float32,
        )

    def reduce_blocks(parts):
        me = lax.axis_index(AXES)
        step = 1
        while step < shards:
            held = parts.shape[1]
            pair = parts.reshape(parts.shape[0], held // 2, 2, *parts.shape[2:])
            upper = (me // step) % 2 == 1
            keep = jnp.where(upper, pair[:, :, 1], pair[:, :, 0])
            send = jnp.where(upper, pair[:, :, 0], pair[:, :, 1])
            if step > 1:
                send = send.astype(jnp.bfloat16)
            moved = lax.ppermute(send, AXES, [(i, i ^ step) for i in range(shards)])
            parts = keep + moved.astype(jnp.float32)
            step *= 2
        return parts[:, 0] / (groups * shards)

    mixed_one, first_matmul_result, whole_one = forward_layer(None, weight_one, spread_in)
    latent_state = (
        jax.nn.silu(first_matmul_result).astype(jnp.bfloat16).reshape(groups, width, depth)
    )
    mixed_two, product_two, whole_two = forward_layer(latent_state, weight_two)
    delta_two = (
        final_layer_sensitivity.reshape(count, depth).astype(jnp.float32) * swish_slope(product_two)
    ).astype(jnp.bfloat16)
    parts_two = grad_parts(mixed_two, delta_two)
    upstream_second = back_weight(delta_two, weight_two)
    fetched_second = (normalizer_factor * upstream_second.reshape(groups, width, depth)).astype(
        jnp.bfloat16
    )
    delta_one = (
        spread_back(link, fetched_second).reshape(count, depth) * swish_slope(first_matmul_result)
    ).astype(jnp.bfloat16)
    parts_one = grad_parts(mixed_one, delta_one)
    upstream_first = back_weight(delta_one, weight_one)
    fetched_first = (normalizer_factor * upstream_first.reshape(groups, width, depth)).astype(
        jnp.bfloat16
    )
    outgoing = lax.dot_general(
        linked_slots,
        fetched_first.reshape(count, depth),
        (((0,), (0,)), ((), ())),
        preferred_element_type=jnp.float32,
    ).astype(jnp.bfloat16)
    returned = exchange(outgoing)
    table_grad = lax.dot_general(
        picks, returned, (((0, 1), (0, 1)), ((), ())), preferred_element_type=jnp.float32
    )
    grad_one = reduce_blocks(parts_one[None])[0].T
    grad_two = reduce_blocks(parts_two[None])[0].T
    return (table_grad, grad_one, grad_two)


def solution(mesh):
    placed = (
        P(AXES, None),
        P(AXES, None),
        P(AXES, None, None),
        P(None, "fsdp"),
        P(None, "fsdp"),
        P(AXES, None, None),
    )
    return jax.shard_map(
        on_device,
        mesh=mesh,
        in_specs=placed,
        out_specs=(P(AXES, None), P(None, AXES), P(None, AXES)),
        check_vma=False,
    )
```

```python
import jax
import jax.numpy as jnp
from jax import lax
from jax.sharding import PartitionSpec as P

AXES = ("node", "fsdp")


def swish_slope(values):
    sigma = jax.nn.sigmoid(values)
    return sigma * (1.0 + values * (1.0 - sigma))


def spread(link, values):
    return jnp.einsum("gij,gjd->gid", link, values, preferred_element_type=jnp.float32)


def spread_back(link, values):
    return jnp.einsum("gji,gjd->gid", link, values, preferred_element_type=jnp.float32)


def exchange(values):
    return lax.all_to_all(values, AXES, 0, 0, tiled=True)


def step_body(
    feature_table, vertex_labels, incidence_mask, weight_one, weight_two, final_layer_sensitivity
):
    groups, width = vertex_labels.shape
    count = groups * width
    n_node = lax.axis_size("node")
    n_fsdp = lax.axis_size("fsdp")
    shards = n_node * n_fsdp
    rows_here = feature_table.shape[0]
    depth = feature_table.shape[1]
    capacity = (2 * count + shards - 1) // shards + 1
    flat_ids = vertex_labels.reshape(count)
    owner = flat_ids // rows_here
    within = flat_ids % rows_here
    one_hot = (owner[:, None] == jnp.arange(shards, dtype=jnp.int32)[None, :]).astype(jnp.int32)
    before = jnp.cumsum(one_hot, axis=0) - one_hot
    rank = jnp.sum(before * one_hot, axis=1)
    position = owner * capacity + rank
    requests = jnp.full((shards * capacity,), -1, jnp.int32).at[position].set(within)
    asked = exchange(requests.reshape(shards, capacity))
    valid = asked >= 0
    safe_rows = jnp.maximum(asked, 0)
    picks = (
        (safe_rows[..., None] == jnp.arange(rows_here, dtype=jnp.int32)) & valid[..., None]
    ).astype(jnp.bfloat16)
    found = jnp.dot(picks, feature_table, preferred_element_type=jnp.float32).astype(jnp.bfloat16)
    answered = exchange(found)
    slot_of = (
        (owner[:, None, None] == jnp.arange(shards, dtype=jnp.int32)[:, None])
        & (rank[:, None, None] == jnp.arange(capacity, dtype=jnp.int32))
    ).astype(jnp.bfloat16)
    degree = jnp.sum(incidence_mask, axis=2).astype(jnp.float32)
    normalizer_factor = lax.rsqrt(1.0 + degree)[..., None]
    link = (incidence_mask + jnp.eye(width, dtype=jnp.int32)[None]).astype(jnp.bfloat16)
    linked_slots = (
        jnp.einsum(
            "gij,gjsc->gisc",
            link,
            slot_of.reshape(groups, width, shards, capacity),
            preferred_element_type=jnp.float32,
        )
        .astype(jnp.bfloat16)
        .reshape(count, shards, capacity)
    )
    spread_in = lax.dot_general(
        linked_slots, answered, (((1, 2), (0, 1)), ((), ())), preferred_element_type=jnp.float32
    )

    def forward_layer(layer_in, weight, spread_done=None):
        if spread_done is None:
            spread_done = spread(link, layer_in)
        mixed = (
            (normalizer_factor * spread_done.reshape(groups, width, depth))
            .astype(jnp.bfloat16)
            .reshape(count, depth)
        )
        product = jnp.dot(
            mixed,
            lax.all_gather(weight, "fsdp", axis=1, tiled=True),
            preferred_element_type=jnp.float32,
        )
        return (mixed, product, weight)

    def back_weight(delta, weight):
        return lax.dot_general(
            delta,
            lax.all_gather(weight, "fsdp", axis=1, tiled=True),
            (((1,), (1,)), ((), ())),
            preferred_element_type=jnp.float32,
        )

    def grad_parts(mixed, delta):
        return lax.dot_general(
            delta.reshape(count, shards, depth // shards),
            mixed,
            (((0,), (0,)), ((), ())),
            preferred_element_type=jnp.float32,
        )

    def reduce_blocks(parts):
        me = lax.axis_index(AXES)
        step = 1
        while step < shards:
            held = parts.shape[1]
            pair = parts.reshape(parts.shape[0], held // 2, 2, *parts.shape[2:])
            upper = (me // step) % 2 == 1
            keep = jnp.where(upper, pair[:, :, 1], pair[:, :, 0])
            send = jnp.where(upper, pair[:, :, 0], pair[:, :, 1])
            send = send.astype(jnp.bfloat16)
            moved = lax.ppermute(send, AXES, [(i, i ^ step) for i in range(shards)])
            parts = keep + moved.astype(jnp.float32)
            step *= 2
        return parts[:, 0] / (groups * shards)

    mixed_one, first_matmul_result, _ = forward_layer(None, weight_one, spread_in)
    latent_state = (
        jax.nn.silu(first_matmul_result).astype(jnp.bfloat16).reshape(groups, width, depth)
    )
    mixed_two, product_two, _ = forward_layer(latent_state, weight_two)
    delta_two = (
        final_layer_sensitivity.reshape(count, depth).astype(jnp.float32) * swish_slope(product_two)
    ).astype(jnp.bfloat16)
    parts_two = grad_parts(mixed_two, delta_two)
    upstream_second = back_weight(delta_two, weight_two)
    fetched_second = (normalizer_factor * upstream_second.reshape(groups, width, depth)).astype(
        jnp.bfloat16
    )
    delta_one = (
        spread_back(link, fetched_second).reshape(count, depth) * swish_slope(first_matmul_result)
    ).astype(jnp.bfloat16)
    parts_one = grad_parts(mixed_one, delta_one)
    upstream_first = back_weight(delta_one, weight_one)
    fetched_first = (normalizer_factor * upstream_first.reshape(groups, width, depth)).astype(
        jnp.bfloat16
    )
    outgoing = lax.dot_general(
        linked_slots,
        fetched_first.reshape(count, depth),
        (((0,), (0,)), ((), ())),
        preferred_element_type=jnp.float32,
    ).astype(jnp.bfloat16)
    returned = exchange(outgoing)
    table_grad = lax.dot_general(
        picks, returned, (((0, 1), (0, 1)), ((), ())), preferred_element_type=jnp.float32
    )
    grad_one = reduce_blocks(parts_one[None])[0].T
    grad_two = reduce_blocks(parts_two[None])[0].T
    return (table_grad, grad_one, grad_two)


def solution(mesh):
    placed = (
        P(AXES, None),
        P(AXES, None),
        P(AXES, None, None),
        P(None, "fsdp"),
        P(None, "fsdp"),
        P(AXES, None, None),
    )
    return jax.shard_map(
        step_body,
        mesh=mesh,
        in_specs=placed,
        out_specs=(P(AXES, None), P(None, AXES), P(None, AXES)),
        check_vma=False,
    )
```

```python
import jax
import jax.numpy as jnp
from jax import lax
from jax.sharding import PartitionSpec as P

AXES = ("node", "fsdp")


def swish_slope(values):
    sigma = jax.nn.sigmoid(values)
    return sigma * (1.0 + values * (1.0 - sigma))


def spread(link, values):
    return jnp.einsum("gij,gjd->gid", link, values, preferred_element_type=jnp.float32)


def spread_back(link, values):
    return jnp.einsum("gji,gjd->gid", link, values, preferred_element_type=jnp.float32)


def exchange(values):
    return lax.all_to_all(values, AXES, 0, 0, tiled=True)


def step_body(
    feature_table, vertex_labels, incidence_mask, weight_one, weight_two, final_layer_sensitivity
):
    groups, width = vertex_labels.shape
    count = groups * width
    n_node = lax.axis_size("node")
    n_fsdp = lax.axis_size("fsdp")
    shards = n_node * n_fsdp
    rows_here = feature_table.shape[0]
    depth = feature_table.shape[1]
    capacity = (2 * count + shards - 1) // shards + 1
    flat_ids = vertex_labels.reshape(count)
    owner = flat_ids // rows_here
    within = flat_ids % rows_here
    one_hot = (owner[:, None] == jnp.arange(shards, dtype=jnp.int32)[None, :]).astype(jnp.int32)
    before = jnp.cumsum(one_hot, axis=0) - one_hot
    rank = jnp.sum(before * one_hot, axis=1)
    position = owner * capacity + rank
    requests = jnp.full((shards * capacity,), -1, jnp.int32).at[position].set(within)
    asked = exchange(requests.reshape(shards, capacity))
    valid = asked >= 0
    safe_rows = jnp.maximum(asked, 0)
    picks = (
        (safe_rows[..., None] == jnp.arange(rows_here, dtype=jnp.int32)) & valid[..., None]
    ).astype(jnp.bfloat16)
    found = jnp.dot(picks, feature_table, preferred_element_type=jnp.float32).astype(jnp.bfloat16)
    answered = exchange(found)
    slot_of = (
        (owner[:, None, None] == jnp.arange(shards, dtype=jnp.int32)[:, None])
        & (rank[:, None, None] == jnp.arange(capacity, dtype=jnp.int32))
    ).astype(jnp.bfloat16)
    degree = jnp.sum(incidence_mask, axis=2).astype(jnp.float32)
    normalizer_factor = lax.rsqrt(1.0 + degree)[..., None]
    link = (incidence_mask + jnp.eye(width, dtype=jnp.int32)[None]).astype(jnp.bfloat16)
    linked_slots = (
        jnp.einsum(
            "gij,gjsc->gisc",
            link,
            slot_of.reshape(groups, width, shards, capacity),
            preferred_element_type=jnp.float32,
        )
        .astype(jnp.bfloat16)
        .reshape(count, shards, capacity)
    )
    spread_in = lax.dot_general(
        linked_slots, answered, (((1, 2), (0, 1)), ((), ())), preferred_element_type=jnp.float32
    )

    def forward_layer(layer_in, weight, spread_done=None):
        if spread_done is None:
            spread_done = spread(link, layer_in)
        mixed = (
            (normalizer_factor * spread_done.reshape(groups, width, depth))
            .astype(jnp.bfloat16)
            .reshape(count, depth)
        )
        product = lax.dot_general(
            mixed, weight, (((1,), (1,)), ((), ())), preferred_element_type=jnp.float32
        ).reshape(count, depth)
        return (mixed, product, weight)

    def back_weight(delta, weight):
        return lax.dot_general(
            delta.reshape(count, n_fsdp, weight.shape[2]),
            weight,
            (((1, 2), (0, 2)), ((), ())),
            preferred_element_type=jnp.float32,
        )

    def gather_columns(weight):
        column = lax.axis_index("fsdp")
        blocks = weight[None]
        step = 1
        while step < n_fsdp:
            other = lax.ppermute(blocks, "fsdp", [(i, i ^ step) for i in range(n_fsdp)])
            upper = (column // step) % 2 == 1
            blocks = jnp.concatenate(
                [jnp.where(upper, other, blocks), jnp.where(upper, blocks, other)], axis=0
            )
            step *= 2
        return blocks

    whole_weight_one = gather_columns(weight_one)
    whole_weight_two = gather_columns(weight_two)

    def grad_parts(mixed, delta):
        return lax.dot_general(
            delta.reshape(count, shards, depth // shards),
            mixed,
            (((0,), (0,)), ((), ())),
            preferred_element_type=jnp.float32,
        )

    def reduce_blocks(parts):
        me = lax.axis_index(AXES)
        step = 1
        while step < shards:
            held = parts.shape[1]
            pair = parts.reshape(parts.shape[0], held // 2, 2, *parts.shape[2:])
            upper = (me // step) % 2 == 1
            keep = jnp.where(upper, pair[:, :, 1], pair[:, :, 0])
            send = jnp.where(upper, pair[:, :, 0], pair[:, :, 1])
            if step > 1:
                send = send.astype(jnp.bfloat16)
            moved = lax.ppermute(send, AXES, [(i, i ^ step) for i in range(shards)])
            parts = keep + moved.astype(jnp.float32)
            step *= 2
        return parts[:, 0] / (groups * shards)

    mixed_one, first_matmul_result, _ = forward_layer(None, whole_weight_one, spread_in)
    latent_state = (
        jax.nn.silu(first_matmul_result).astype(jnp.bfloat16).reshape(groups, width, depth)
    )
    mixed_two, product_two, _ = forward_layer(latent_state, whole_weight_two)
    delta_two = (
        final_layer_sensitivity.reshape(count, depth).astype(jnp.float32) * swish_slope(product_two)
    ).astype(jnp.bfloat16)
    parts_two = grad_parts(mixed_two, delta_two)
    upstream_second = back_weight(delta_two, whole_weight_two)
    fetched_second = (normalizer_factor * upstream_second.reshape(groups, width, depth)).astype(
        jnp.bfloat16
    )
    delta_one = (
        spread_back(link, fetched_second).reshape(count, depth) * swish_slope(first_matmul_result)
    ).astype(jnp.bfloat16)
    parts_one = grad_parts(mixed_one, delta_one)
    upstream_first = back_weight(delta_one, whole_weight_one)
    fetched_first = (normalizer_factor * upstream_first.reshape(groups, width, depth)).astype(
        jnp.bfloat16
    )
    outgoing = lax.dot_general(
        linked_slots,
        fetched_first.reshape(count, depth),
        (((0,), (0,)), ((), ())),
        preferred_element_type=jnp.float32,
    ).astype(jnp.bfloat16)
    returned = exchange(outgoing)
    table_grad = lax.dot_general(
        picks, returned, (((0, 1), (0, 1)), ((), ())), preferred_element_type=jnp.float32
    )
    grad_one = reduce_blocks(parts_one[None])[0].T
    grad_two = reduce_blocks(parts_two[None])[0].T
    return (table_grad, grad_one, grad_two)


def solution(mesh):
    placed = (
        P(AXES, None),
        P(AXES, None),
        P(AXES, None, None),
        P(None, "fsdp"),
        P(None, "fsdp"),
        P(AXES, None, None),
    )
    return jax.shard_map(
        step_body,
        mesh=mesh,
        in_specs=placed,
        out_specs=(P(AXES, None), P(None, AXES), P(None, AXES)),
        check_vma=False,
    )
```

```python
import jax
import jax.numpy as jnp
from jax import lax
from jax.sharding import PartitionSpec as P

AXES = ("node", "fsdp")


def swish_slope(values):
    sigma = jax.nn.sigmoid(values)
    return sigma * (1.0 + values * (1.0 - sigma))


def spread(link, values):
    return jnp.einsum("gij,gjd->gid", link, values, preferred_element_type=jnp.float32)


def spread_back(link, values):
    return jnp.einsum("gji,gjd->gid", link, values, preferred_element_type=jnp.float32)


def exchange(values):
    return lax.all_to_all(values, AXES, 0, 0, tiled=True)


def step_body(
    feature_table, vertex_labels, incidence_mask, weight_one, weight_two, final_layer_sensitivity
):
    groups, width = vertex_labels.shape
    count = groups * width
    n_node = lax.axis_size("node")
    n_fsdp = lax.axis_size("fsdp")
    shards = n_node * n_fsdp
    rows_here = feature_table.shape[0]
    depth = feature_table.shape[1]
    capacity = (2 * count + shards - 1) // shards + 1
    flat_ids = vertex_labels.reshape(count)
    owner = flat_ids // rows_here
    within = flat_ids % rows_here
    one_hot = (owner[:, None] == jnp.arange(shards, dtype=jnp.int32)[None, :]).astype(jnp.int32)
    before = jnp.cumsum(one_hot, axis=0) - one_hot
    rank = jnp.sum(before * one_hot, axis=1)
    position = owner * capacity + rank
    requests = jnp.full((shards * capacity,), -1, jnp.int32).at[position].set(within)
    asked = exchange(requests.reshape(shards, capacity))
    valid = asked >= 0
    safe_rows = jnp.maximum(asked, 0)
    picks = (
        (safe_rows[..., None] == jnp.arange(rows_here, dtype=jnp.int32)) & valid[..., None]
    ).astype(jnp.bfloat16)
    found = jnp.dot(picks, feature_table, preferred_element_type=jnp.float32).astype(jnp.bfloat16)
    answered = exchange(found)
    slot_of = (
        (owner[:, None, None] == jnp.arange(shards, dtype=jnp.int32)[:, None])
        & (rank[:, None, None] == jnp.arange(capacity, dtype=jnp.int32))
    ).astype(jnp.bfloat16)
    degree = jnp.sum(incidence_mask, axis=2).astype(jnp.float32)
    normalizer_factor = lax.rsqrt(1.0 + degree)[..., None]
    link = (incidence_mask + jnp.eye(width, dtype=jnp.int32)[None]).astype(jnp.bfloat16)
    linked_slots = (
        jnp.einsum(
            "gij,gjsc->gisc",
            link,
            slot_of.reshape(groups, width, shards, capacity),
            preferred_element_type=jnp.float32,
        )
        .astype(jnp.bfloat16)
        .reshape(count, shards, capacity)
    )
    spread_in = lax.dot_general(
        linked_slots, answered, (((1, 2), (0, 1)), ((), ())), preferred_element_type=jnp.float32
    )

    def forward_layer(layer_in, weight, spread_done=None):
        if spread_done is None:
            spread_done = spread(link, layer_in)
        mixed = (
            (normalizer_factor * spread_done.reshape(groups, width, depth))
            .astype(jnp.bfloat16)
            .reshape(count, depth)
        )
        product = lax.dot_general(
            mixed, weight, (((1,), (1,)), ((), ())), preferred_element_type=jnp.float32
        ).reshape(count, depth)
        return (mixed, product, weight)

    def back_weight(delta, weight):
        return lax.dot_general(
            delta.reshape(count, n_fsdp, weight.shape[2]),
            weight,
            (((1, 2), (0, 2)), ((), ())),
            preferred_element_type=jnp.float32,
        )

    def gather_columns(weight):
        column = lax.axis_index("fsdp")
        blocks = weight[None]
        step = n_fsdp // 2
        while step >= 1:
            other = lax.ppermute(blocks, "fsdp", [(i, i ^ step) for i in range(n_fsdp)])
            upper = (column // step) % 2 == 1
            blocks = jnp.concatenate(
                [jnp.where(upper, other, blocks), jnp.where(upper, blocks, other)], axis=0
            )
            step //= 2
        bits = n_fsdp.bit_length() - 1
        blocks = blocks.reshape((2,) * bits + weight.shape)
        blocks = blocks.transpose(tuple(range(bits))[::-1] + (bits, bits + 1))
        return blocks.reshape((n_fsdp,) + weight.shape)

    whole_weight_one = gather_columns(weight_one)
    whole_weight_two = gather_columns(weight_two)

    def grad_parts(mixed, delta):
        return lax.dot_general(
            delta.reshape(count, shards, depth // shards),
            mixed,
            (((0,), (0,)), ((), ())),
            preferred_element_type=jnp.float32,
        )

    def reduce_blocks(parts):
        me = lax.axis_index(AXES)
        step = 1
        while step < shards:
            held = parts.shape[1]
            pair = parts.reshape(parts.shape[0], held // 2, 2, *parts.shape[2:])
            upper = (me // step) % 2 == 1
            keep = jnp.where(upper, pair[:, :, 1], pair[:, :, 0])
            send = jnp.where(upper, pair[:, :, 0], pair[:, :, 1])
            if step > 1:
                send = send.astype(jnp.bfloat16)
            moved = lax.ppermute(send, AXES, [(i, i ^ step) for i in range(shards)])
            parts = keep + moved.astype(jnp.float32)
            step *= 2
        return parts[:, 0] / (groups * shards)

    mixed_one, first_matmul_result, _ = forward_layer(None, whole_weight_one, spread_in)
    latent_state = (
        jax.nn.silu(first_matmul_result).astype(jnp.bfloat16).reshape(groups, width, depth)
    )
    mixed_two, product_two, _ = forward_layer(latent_state, whole_weight_two)
    delta_two = (
        final_layer_sensitivity.reshape(count, depth).astype(jnp.float32) * swish_slope(product_two)
    ).astype(jnp.bfloat16)
    parts_two = grad_parts(mixed_two, delta_two)
    upstream_second = back_weight(delta_two, whole_weight_two)
    fetched_second = (normalizer_factor * upstream_second.reshape(groups, width, depth)).astype(
        jnp.bfloat16
    )
    delta_one = (
        spread_back(link, fetched_second).reshape(count, depth) * swish_slope(first_matmul_result)
    ).astype(jnp.bfloat16)
    parts_one = grad_parts(mixed_one, delta_one)
    upstream_first = back_weight(delta_one, whole_weight_one)
    fetched_first = (normalizer_factor * upstream_first.reshape(groups, width, depth)).astype(
        jnp.bfloat16
    )
    outgoing = lax.dot_general(
        linked_slots,
        fetched_first.reshape(count, depth),
        (((0,), (0,)), ((), ())),
        preferred_element_type=jnp.float32,
    ).astype(jnp.bfloat16)
    returned = exchange(outgoing)
    table_grad = lax.dot_general(
        picks, returned, (((0, 1), (0, 1)), ((), ())), preferred_element_type=jnp.float32
    )
    grad_one = reduce_blocks(parts_one[None])[0].T
    grad_two = reduce_blocks(parts_two[None])[0].T
    return (table_grad, grad_one, grad_two)


def solution(mesh):
    placed = (
        P(AXES, None),
        P(AXES, None),
        P(AXES, None, None),
        P(None, "fsdp"),
        P(None, "fsdp"),
        P(AXES, None, None),
    )
    return jax.shard_map(
        step_body,
        mesh=mesh,
        in_specs=placed,
        out_specs=(P(AXES, None), P(None, AXES), P(None, AXES)),
        check_vma=False,
    )
```

```python
import jax
import jax.numpy as jnp
from jax import lax
from jax.sharding import PartitionSpec as P

AXES = ("node", "fsdp")


def swish_slope(values):
    sigma = jax.nn.sigmoid(values)
    return sigma * (1.0 + values * (1.0 - sigma))


def spread(link, values):
    return jnp.einsum("gij,gjd->gid", link, values, preferred_element_type=jnp.float32)


def spread_back(link, values):
    return jnp.einsum("gji,gjd->gid", link, values, preferred_element_type=jnp.float32)


def exchange(values):
    return lax.all_to_all(values, AXES, 0, 0, tiled=True)


def step_body(
    feature_table, vertex_labels, incidence_mask, weight_one, weight_two, final_layer_sensitivity
):
    groups, width = vertex_labels.shape
    count = groups * width
    n_node = lax.axis_size("node")
    n_fsdp = lax.axis_size("fsdp")
    shards = n_node * n_fsdp
    rows_here = feature_table.shape[0]
    depth = feature_table.shape[1]
    capacity = (2 * count + shards - 1) // shards + 1
    flat_ids = vertex_labels.reshape(count)
    owner = flat_ids // rows_here
    within = flat_ids % rows_here
    one_hot = (owner[:, None] == jnp.arange(shards, dtype=jnp.int32)[None, :]).astype(jnp.int32)
    before = jnp.cumsum(one_hot, axis=0) - one_hot
    rank = jnp.sum(before * one_hot, axis=1)
    position = owner * capacity + rank
    requests = jnp.full((shards * capacity,), -1, jnp.int32).at[position].set(within)
    asked = exchange(requests.reshape(shards, capacity))
    valid = asked >= 0
    safe_rows = jnp.maximum(asked, 0)
    picks = (
        (safe_rows[..., None] == jnp.arange(rows_here, dtype=jnp.int32)) & valid[..., None]
    ).astype(jnp.bfloat16)
    found = jnp.dot(picks, feature_table, preferred_element_type=jnp.float32).astype(jnp.bfloat16)
    answered = exchange(found)
    slot_of = (
        (owner[:, None, None] == jnp.arange(shards, dtype=jnp.int32)[:, None])
        & (rank[:, None, None] == jnp.arange(capacity, dtype=jnp.int32))
    ).astype(jnp.bfloat16)
    degree = jnp.sum(incidence_mask, axis=2).astype(jnp.float32)
    normalizer_factor = lax.rsqrt(1.0 + degree)[..., None]
    link = (incidence_mask + jnp.eye(width, dtype=jnp.int32)[None]).astype(jnp.bfloat16)
    linked_slots = (
        jnp.einsum(
            "gij,gjsc->gisc",
            link,
            slot_of.reshape(groups, width, shards, capacity),
            preferred_element_type=jnp.float32,
        )
        .astype(jnp.bfloat16)
        .reshape(count, shards, capacity)
    )
    spread_in = lax.dot_general(
        linked_slots, answered, (((1, 2), (0, 1)), ((), ())), preferred_element_type=jnp.float32
    )

    def forward_layer(layer_in, weight, spread_done=None):
        if spread_done is None:
            spread_done = spread(link, layer_in)
        mixed = (
            (normalizer_factor * spread_done.reshape(groups, width, depth))
            .astype(jnp.bfloat16)
            .reshape(count, depth)
        )
        product = lax.dot_general(
            mixed, weight, (((1,), (1,)), ((), ())), preferred_element_type=jnp.float32
        ).reshape(count, depth)
        return (mixed, product, weight)

    def back_weight(delta, weight):
        return lax.dot_general(
            delta.reshape(count, n_fsdp, weight.shape[2]),
            weight,
            (((1, 2), (0, 2)), ((), ())),
            preferred_element_type=jnp.float32,
        )

    def gather_columns(weight):
        column = lax.axis_index("fsdp")
        blocks = weight[None]
        step = n_fsdp // 2
        while step >= 1:
            other = lax.ppermute(blocks, "fsdp", [(i, i ^ step) for i in range(n_fsdp)])
            upper = (column // step) % 2 == 1
            blocks = jnp.concatenate(
                [jnp.where(upper, other, blocks), jnp.where(upper, blocks, other)], axis=0
            )
            step //= 2
        bits = n_fsdp.bit_length() - 1
        blocks = blocks.reshape((2,) * bits + weight.shape)
        blocks = blocks.transpose(tuple(range(bits))[::-1] + (bits, bits + 1))
        return blocks.reshape((n_fsdp,) + weight.shape)

    whole_weight_one = gather_columns(weight_one)
    whole_weight_two = gather_columns(weight_two)

    def grad_parts(mixed, delta):
        return lax.dot_general(
            delta.reshape(count, shards, depth // shards),
            mixed,
            (((0,), (0,)), ((), ())),
            preferred_element_type=jnp.float32,
        )

    def reduce_blocks(parts):
        me = lax.axis_index(AXES)
        step = 1
        while step < shards:
            held = parts.shape[1]
            pair = parts.reshape(parts.shape[0], held // 2, 2, *parts.shape[2:])
            upper = (me // step) % 2 == 1
            keep = jnp.where(upper, pair[:, :, 1], pair[:, :, 0])
            send = jnp.where(upper, pair[:, :, 0], pair[:, :, 1])
            if step > 1:
                send = send.astype(jnp.bfloat16)
            moved = lax.ppermute(send, AXES, [(i, i ^ step) for i in range(shards)])
            parts = keep + moved.astype(jnp.float32)
            step *= 2
        return parts[:, 0] / (groups * shards)

    mixed_one, first_matmul_result, _ = forward_layer(None, whole_weight_one, spread_in)
    latent_state = (
        jax.nn.silu(first_matmul_result).astype(jnp.bfloat16).reshape(groups, width, depth)
    )
    mixed_two, product_two, _ = forward_layer(latent_state, whole_weight_two)
    delta_two = (
        final_layer_sensitivity.reshape(count, depth).astype(jnp.float32) * swish_slope(product_two)
    ).astype(jnp.bfloat16)
    parts_two = grad_parts(mixed_two, delta_two)
    upstream_second = back_weight(delta_two, whole_weight_two)
    fetched_second = (normalizer_factor * upstream_second.reshape(groups, width, depth)).astype(
        jnp.bfloat16
    )
    delta_one = (
        spread_back(link, fetched_second).reshape(count, depth) * swish_slope(first_matmul_result)
    ).astype(jnp.bfloat16)
    parts_one = grad_parts(mixed_one, delta_one)
    upstream_first = back_weight(delta_one, whole_weight_one)
    fetched_first = (normalizer_factor * upstream_first.reshape(groups, width, depth)).astype(
        jnp.bfloat16
    )
    input_grad = spread_back(link, fetched_first).astype(jnp.bfloat16).reshape(count, depth)
    outgoing = lax.dot_general(
        slot_of, input_grad, (((0,), (0,)), ((), ())), preferred_element_type=jnp.float32
    ).astype(jnp.bfloat16)
    returned = exchange(outgoing)
    table_grad = lax.dot_general(
        picks, returned, (((0, 1), (0, 1)), ((), ())), preferred_element_type=jnp.float32
    )
    grad_one = reduce_blocks(parts_one[None])[0].T
    grad_two = reduce_blocks(parts_two[None])[0].T
    return (table_grad, grad_one, grad_two)


def solution(mesh):
    placed = (
        P(AXES, None),
        P(AXES, None),
        P(AXES, None, None),
        P(None, "fsdp"),
        P(None, "fsdp"),
        P(AXES, None, None),
    )
    return jax.shard_map(
        step_body,
        mesh=mesh,
        in_specs=placed,
        out_specs=(P(AXES, None), P(None, AXES), P(None, AXES)),
        check_vma=False,
    )
```

```python
import jax
import jax.numpy as jnp
from jax import lax
from jax.sharding import PartitionSpec as P

AXES = ("node", "fsdp")


def swish_slope(values):
    sigma = jax.nn.sigmoid(values)
    return sigma * (1.0 + values * (1.0 - sigma))


def spread(link, values):
    return jnp.einsum("gij,gjd->gid", link, values, preferred_element_type=jnp.float32)


def spread_back(link, values):
    return jnp.einsum("gji,gjd->gid", link, values, preferred_element_type=jnp.float32)


def exchange(values):
    return lax.all_to_all(values, AXES, 0, 0, tiled=True)


def step_body(
    feature_table, vertex_labels, incidence_mask, weight_one, weight_two, final_layer_sensitivity
):
    groups, width = vertex_labels.shape
    count = groups * width
    n_node = lax.axis_size("node")
    n_fsdp = lax.axis_size("fsdp")
    shards = n_node * n_fsdp
    rows_here = feature_table.shape[0]
    depth = feature_table.shape[1]
    capacity = (2 * count + shards - 1) // shards + 1
    flat_ids = vertex_labels.reshape(count)
    owner = flat_ids // rows_here
    within = flat_ids % rows_here
    one_hot = (owner[:, None] == jnp.arange(shards, dtype=jnp.int32)[None, :]).astype(jnp.int32)
    before = jnp.cumsum(one_hot, axis=0) - one_hot
    rank = jnp.sum(before * one_hot, axis=1)
    position = owner * capacity + rank
    requests = jnp.full((shards * capacity,), -1, jnp.int32).at[position].set(within)
    asked = exchange(requests.reshape(shards, capacity))
    valid = asked >= 0
    safe_rows = jnp.maximum(asked, 0)
    picks = (
        (safe_rows[..., None] == jnp.arange(rows_here, dtype=jnp.int32)) & valid[..., None]
    ).astype(jnp.bfloat16)
    found = jnp.dot(picks, feature_table, preferred_element_type=jnp.float32).astype(jnp.bfloat16)
    answered = exchange(found)
    slot_of = (
        (owner[:, None, None] == jnp.arange(shards, dtype=jnp.int32)[:, None])
        & (rank[:, None, None] == jnp.arange(capacity, dtype=jnp.int32))
    ).astype(jnp.bfloat16)
    degree = jnp.sum(incidence_mask, axis=2).astype(jnp.float32)
    normalizer_factor = lax.rsqrt(1.0 + degree)[..., None]
    link = (incidence_mask + jnp.eye(width, dtype=jnp.int32)[None]).astype(jnp.bfloat16)
    linked_slots = (
        jnp.einsum(
            "gij,gjsc->gisc",
            link,
            slot_of.reshape(groups, width, shards, capacity),
            preferred_element_type=jnp.float32,
        )
        .astype(jnp.bfloat16)
        .reshape(count, shards, capacity)
    )
    spread_in = lax.dot_general(
        linked_slots, answered, (((1, 2), (0, 1)), ((), ())), preferred_element_type=jnp.float32
    )

    def forward_layer(layer_in, weight, spread_done=None):
        if spread_done is None:
            spread_done = spread(link, layer_in)
        mixed = (
            (normalizer_factor * spread_done.reshape(groups, width, depth))
            .astype(jnp.bfloat16)
            .reshape(count, depth)
        )
        product = lax.dot_general(
            mixed, weight, (((1,), (1,)), ((), ())), preferred_element_type=jnp.float32
        ).reshape(count, depth)
        return (mixed, product, weight)

    def back_weight(delta, weight):
        return lax.dot_general(
            delta.reshape(count, n_fsdp, weight.shape[2]),
            weight,
            (((1, 2), (0, 2)), ((), ())),
            preferred_element_type=jnp.float32,
        )

    def gather_columns(weight):
        column = lax.axis_index("fsdp")
        blocks = weight[None]
        step = n_fsdp // 2
        while step >= 1:
            other = lax.ppermute(blocks, "fsdp", [(i, i ^ step) for i in range(n_fsdp)])
            upper = (column // step) % 2 == 1
            blocks = jnp.concatenate(
                [jnp.where(upper, other, blocks), jnp.where(upper, blocks, other)], axis=0
            )
            step //= 2
        bits = n_fsdp.bit_length() - 1
        blocks = blocks.reshape((2,) * bits + weight.shape)
        blocks = blocks.transpose(tuple(range(bits))[::-1] + (bits, bits + 1))
        return blocks.reshape((n_fsdp,) + weight.shape)

    whole_weight_one = gather_columns(weight_one)
    whole_weight_two = gather_columns(weight_two)

    def grad_parts(mixed, delta):
        return lax.dot_general(
            delta.reshape(count, shards, depth // shards),
            mixed,
            (((0,), (0,)), ((), ())),
            preferred_element_type=jnp.float32,
        )

    def reduce_blocks(parts, order):
        me = lax.axis_index(AXES)
        bits = len(order)
        axes = [1 + (bits - 1 - order[t]) for t in reversed(range(bits))]
        parts = parts.reshape((parts.shape[0],) + (2,) * bits + parts.shape[2:])
        parts = parts.transpose([0] + axes + [bits + 1, bits + 2])
        parts = parts.reshape((parts.shape[0], shards) + parts.shape[bits + 1 :])
        for t, bit in enumerate(order):
            step = 1 << bit
            held = parts.shape[1]
            pair = parts.reshape(parts.shape[0], held // 2, 2, *parts.shape[2:])
            upper = (me // step) % 2 == 1
            keep = jnp.where(upper, pair[:, :, 1], pair[:, :, 0])
            send = jnp.where(upper, pair[:, :, 0], pair[:, :, 1])
            if t > 0:
                send = send.astype(jnp.bfloat16)
            moved = lax.ppermute(send, AXES, [(i, i ^ step) for i in range(shards)])
            parts = keep + moved.astype(jnp.float32)
        return parts[:, 0] / (groups * shards)

    mixed_one, first_matmul_result, _ = forward_layer(None, whole_weight_one, spread_in)
    latent_state = (
        jax.nn.silu(first_matmul_result).astype(jnp.bfloat16).reshape(groups, width, depth)
    )
    mixed_two, product_two, _ = forward_layer(latent_state, whole_weight_two)
    delta_two = (
        final_layer_sensitivity.reshape(count, depth).astype(jnp.float32) * swish_slope(product_two)
    ).astype(jnp.bfloat16)
    parts_two = grad_parts(mixed_two, delta_two)
    upstream_second = back_weight(delta_two, whole_weight_two)
    fetched_second = (normalizer_factor * upstream_second.reshape(groups, width, depth)).astype(
        jnp.bfloat16
    )
    delta_one = (
        spread_back(link, fetched_second).reshape(count, depth) * swish_slope(first_matmul_result)
    ).astype(jnp.bfloat16)
    parts_one = grad_parts(mixed_one, delta_one)
    upstream_first = back_weight(delta_one, whole_weight_one)
    fetched_first = (normalizer_factor * upstream_first.reshape(groups, width, depth)).astype(
        jnp.bfloat16
    )
    outgoing = lax.dot_general(
        linked_slots,
        fetched_first.reshape(count, depth),
        (((0,), (0,)), ((), ())),
        preferred_element_type=jnp.float32,
    ).astype(jnp.bfloat16)
    returned = exchange(outgoing)
    table_grad = lax.dot_general(
        picks, returned, (((0, 1), (0, 1)), ((), ())), preferred_element_type=jnp.float32
    )
    bit_order = list(range(shards.bit_length() - 1))
    swapped = list(bit_order)
    cross = n_fsdp.bit_length() - 1
    if 1 < cross < len(swapped):
        swapped[1], swapped[cross] = swapped[cross], swapped[1]
    grad_one = reduce_blocks(parts_one[None], bit_order)[0].T
    grad_two = reduce_blocks(parts_two[None], swapped)[0].T
    return (table_grad, grad_one, grad_two)


def solution(mesh):
    placed = (
        P(AXES, None),
        P(AXES, None),
        P(AXES, None, None),
        P(None, "fsdp"),
        P(None, "fsdp"),
        P(AXES, None, None),
    )
    return jax.shard_map(
        step_body,
        mesh=mesh,
        in_specs=placed,
        out_specs=(P(AXES, None), P(None, AXES), P(None, AXES)),
        check_vma=False,
    )
```

```python
import jax
import jax.numpy as jnp
from jax import lax
from jax.sharding import PartitionSpec as P

AXES = ("node", "fsdp")


def swish_slope(values):
    sigma = jax.nn.sigmoid(values)
    return sigma * (1.0 + values * (1.0 - sigma))


def spread(link, values):
    return jnp.einsum("gij,gjd->gid", link, values, preferred_element_type=jnp.float32)


def spread_back(link, values):
    return jnp.einsum("gji,gjd->gid", link, values, preferred_element_type=jnp.float32)


def exchange(values):
    return lax.all_to_all(values, AXES, 0, 0, tiled=True)


def step_body(
    feature_table, vertex_labels, incidence_mask, weight_one, weight_two, final_layer_sensitivity
):
    groups, width = vertex_labels.shape
    count = groups * width
    n_node = lax.axis_size("node")
    n_fsdp = lax.axis_size("fsdp")
    shards = n_node * n_fsdp
    rows_here = feature_table.shape[0]
    depth = feature_table.shape[1]
    capacity = (2 * count + shards - 1) // shards + 1
    flat_ids = vertex_labels.reshape(count)
    owner = flat_ids // rows_here
    within = flat_ids % rows_here
    one_hot = (owner[:, None] == jnp.arange(shards, dtype=jnp.int32)[None, :]).astype(jnp.int32)
    before = jnp.cumsum(one_hot, axis=0) - one_hot
    rank = jnp.sum(before * one_hot, axis=1)
    position = owner * capacity + rank
    requests = jnp.full((shards * capacity,), -1, jnp.int32).at[position].set(within)
    asked = exchange(requests.reshape(shards, capacity))
    valid = asked >= 0
    safe_rows = jnp.maximum(asked, 0)
    picks = (
        (safe_rows[..., None] == jnp.arange(rows_here, dtype=jnp.int32)) & valid[..., None]
    ).astype(jnp.bfloat16)
    found = jnp.dot(picks, feature_table, preferred_element_type=jnp.float32).astype(jnp.bfloat16)
    answered = exchange(found)
    slot_of = (
        (owner[:, None, None] == jnp.arange(shards, dtype=jnp.int32)[:, None])
        & (rank[:, None, None] == jnp.arange(capacity, dtype=jnp.int32))
    ).astype(jnp.bfloat16)
    degree = jnp.sum(incidence_mask, axis=2).astype(jnp.float32)
    normalizer_factor = lax.rsqrt(1.0 + degree)[..., None]
    link = (incidence_mask + jnp.eye(width, dtype=jnp.int32)[None]).astype(jnp.bfloat16)
    linked_slots = (
        jnp.einsum(
            "gij,gjsc->gisc",
            link,
            slot_of.reshape(groups, width, shards, capacity),
            preferred_element_type=jnp.float32,
        )
        .astype(jnp.bfloat16)
        .reshape(count, shards, capacity)
    )
    spread_in = lax.dot_general(
        linked_slots, answered, (((1, 2), (0, 1)), ((), ())), preferred_element_type=jnp.float32
    )

    def forward_layer(layer_in, weight, spread_done=None):
        if spread_done is None:
            spread_done = spread(link, layer_in)
        mixed = (
            (normalizer_factor * spread_done.reshape(groups, width, depth))
            .astype(jnp.bfloat16)
            .reshape(count, depth)
        )
        product = jnp.dot(mixed, weight, preferred_element_type=jnp.float32)
        return (mixed, product, weight)

    def back_weight(delta, weight):
        return lax.dot_general(
            delta, weight, (((1,), (1,)), ((), ())), preferred_element_type=jnp.float32
        )

    def gather_columns(weight):
        column = lax.axis_index("fsdp")
        blocks = weight[None]
        step = n_fsdp // 2
        while step >= 1:
            other = lax.ppermute(blocks, "fsdp", [(i, i ^ step) for i in range(n_fsdp)])
            upper = (column // step) % 2 == 1
            blocks = jnp.concatenate(
                [jnp.where(upper, other, blocks), jnp.where(upper, blocks, other)], axis=0
            )
            step //= 2
        bits = n_fsdp.bit_length() - 1
        blocks = blocks.reshape((2,) * bits + weight.shape)
        blocks = blocks.transpose(tuple(range(bits))[::-1] + (bits, bits + 1))
        blocks = blocks.reshape((n_fsdp,) + weight.shape)
        return blocks.transpose(1, 0, 2).reshape(weight.shape[0], n_fsdp * weight.shape[1])

    whole_weight_one = gather_columns(weight_one)
    whole_weight_two = gather_columns(weight_two)

    def grad_parts(mixed, delta):
        return lax.dot_general(
            delta.reshape(count, shards, depth // shards),
            mixed,
            (((0,), (0,)), ((), ())),
            preferred_element_type=jnp.float32,
        )

    def reduce_blocks(parts):
        me = lax.axis_index(AXES)
        step = 1
        while step < shards:
            held = parts.shape[1]
            pair = parts.reshape(parts.shape[0], held // 2, 2, *parts.shape[2:])
            upper = (me // step) % 2 == 1
            keep = jnp.where(upper, pair[:, :, 1], pair[:, :, 0])
            send = jnp.where(upper, pair[:, :, 0], pair[:, :, 1])
            if step > 1:
                send = send.astype(jnp.bfloat16)
            moved = lax.ppermute(send, AXES, [(i, i ^ step) for i in range(shards)])
            parts = keep + moved.astype(jnp.float32)
            step *= 2
        return parts[:, 0] / (groups * shards)

    mixed_one, first_matmul_result, _ = forward_layer(None, whole_weight_one, spread_in)
    latent_state = (
        jax.nn.silu(first_matmul_result).astype(jnp.bfloat16).reshape(groups, width, depth)
    )
    mixed_two, product_two, _ = forward_layer(latent_state, whole_weight_two)
    delta_two = (
        final_layer_sensitivity.reshape(count, depth).astype(jnp.float32) * swish_slope(product_two)
    ).astype(jnp.bfloat16)
    parts_two = grad_parts(mixed_two, delta_two)
    upstream_second = back_weight(delta_two, whole_weight_two)
    fetched_second = (normalizer_factor * upstream_second.reshape(groups, width, depth)).astype(
        jnp.bfloat16
    )
    delta_one = (
        spread_back(link, fetched_second).reshape(count, depth) * swish_slope(first_matmul_result)
    ).astype(jnp.bfloat16)
    parts_one = grad_parts(mixed_one, delta_one)
    upstream_first = back_weight(delta_one, whole_weight_one)
    fetched_first = (normalizer_factor * upstream_first.reshape(groups, width, depth)).astype(
        jnp.bfloat16
    )
    outgoing = lax.dot_general(
        linked_slots,
        fetched_first.reshape(count, depth),
        (((0,), (0,)), ((), ())),
        preferred_element_type=jnp.float32,
    ).astype(jnp.bfloat16)
    returned = exchange(outgoing)
    table_grad = lax.dot_general(
        picks, returned, (((0, 1), (0, 1)), ((), ())), preferred_element_type=jnp.float32
    )
    grad_one = reduce_blocks(parts_one[None])[0].T
    grad_two = reduce_blocks(parts_two[None])[0].T
    return (table_grad, grad_one, grad_two)


def solution(mesh):
    placed = (
        P(AXES, None),
        P(AXES, None),
        P(AXES, None, None),
        P(None, "fsdp"),
        P(None, "fsdp"),
        P(AXES, None, None),
    )
    return jax.shard_map(
        step_body,
        mesh=mesh,
        in_specs=placed,
        out_specs=(P(AXES, None), P(None, AXES), P(None, AXES)),
        check_vma=False,
    )
```

```python
import jax
import jax.numpy as jnp
from jax import lax
from jax.sharding import PartitionSpec as P

AXES = ("node", "fsdp")


def swish_slope(values):
    sigma = jax.nn.sigmoid(values)
    return sigma * (1.0 + values * (1.0 - sigma))


def spread(link, values):
    return jnp.einsum("gij,gjd->gid", link, values, preferred_element_type=jnp.float32)


def spread_back(link, values):
    return jnp.einsum("gji,gjd->gid", link, values, preferred_element_type=jnp.float32)


def exchange(values):
    return lax.all_to_all(values, AXES, 0, 0, tiled=True)


def step_body(
    feature_table, vertex_labels, incidence_mask, weight_one, weight_two, final_layer_sensitivity
):
    groups, width = vertex_labels.shape
    count = groups * width
    n_node = lax.axis_size("node")
    n_fsdp = lax.axis_size("fsdp")
    shards = n_node * n_fsdp
    rows_here = feature_table.shape[0]
    depth = feature_table.shape[1]
    capacity = (2 * count + shards - 1) // shards + 1
    flat_ids = vertex_labels.reshape(count)
    owner = flat_ids // rows_here
    within = flat_ids % rows_here
    one_hot = (owner[:, None] == jnp.arange(shards, dtype=jnp.int32)[None, :]).astype(jnp.int32)
    before = jnp.cumsum(one_hot, axis=0) - one_hot
    rank = jnp.sum(before * one_hot, axis=1)
    position = owner * capacity + rank
    requests = jnp.full((shards * capacity,), -1, jnp.int32).at[position].set(within)
    asked = exchange(requests.reshape(shards, capacity))
    valid = asked >= 0
    safe_rows = jnp.maximum(asked, 0)
    picks = (
        (safe_rows[..., None] == jnp.arange(rows_here, dtype=jnp.int32)) & valid[..., None]
    ).astype(jnp.bfloat16)
    found = jnp.dot(picks, feature_table, preferred_element_type=jnp.float32).astype(jnp.bfloat16)
    answered = exchange(found)
    slot_of = (
        (owner[:, None, None] == jnp.arange(shards, dtype=jnp.int32)[:, None])
        & (rank[:, None, None] == jnp.arange(capacity, dtype=jnp.int32))
    ).astype(jnp.bfloat16)
    degree = jnp.sum(incidence_mask, axis=2).astype(jnp.float32)
    normalizer_factor = lax.rsqrt(1.0 + degree)[..., None]
    link = (incidence_mask + jnp.eye(width, dtype=jnp.int32)[None]).astype(jnp.bfloat16)
    linked_slots = (
        jnp.einsum(
            "gij,gjsc->gisc",
            link,
            slot_of.reshape(groups, width, shards, capacity),
            preferred_element_type=jnp.float32,
        )
        .astype(jnp.bfloat16)
        .reshape(count, shards, capacity)
    )
    spread_in = lax.dot_general(
        linked_slots, answered, (((1, 2), (0, 1)), ((), ())), preferred_element_type=jnp.float32
    )

    def forward_layer(layer_in, weight, spread_done=None):
        if spread_done is None:
            spread_done = spread(link, layer_in)
        mixed = (
            (normalizer_factor * spread_done.reshape(groups, width, depth))
            .astype(jnp.bfloat16)
            .reshape(count, depth)
        )
        product = jnp.dot(mixed, weight, preferred_element_type=jnp.float32)
        return (mixed, product, weight)

    def back_weight(delta, weight):
        return lax.dot_general(
            delta, weight, (((1,), (1,)), ((), ())), preferred_element_type=jnp.float32
        )

    def gather_columns(weight):
        column = lax.axis_index("fsdp")
        blocks = weight[None]
        step = n_fsdp // 2
        while step >= 1:
            other = lax.ppermute(blocks, "fsdp", [(i, i ^ step) for i in range(n_fsdp)])
            upper = (column // step) % 2 == 1
            blocks = jnp.concatenate(
                [jnp.where(upper, other, blocks), jnp.where(upper, blocks, other)], axis=0
            )
            step //= 2
        bits = n_fsdp.bit_length() - 1
        blocks = blocks.reshape((2,) * bits + weight.shape)
        blocks = blocks.transpose(tuple(range(bits))[::-1] + (bits, bits + 1))
        blocks = blocks.reshape((n_fsdp,) + weight.shape)
        return blocks.transpose(1, 0, 2).reshape(weight.shape[0], n_fsdp * weight.shape[1])

    whole_weight_one = gather_columns(weight_one)
    whole_weight_two = gather_columns(weight_two)

    def grad_parts(mixed, delta):
        whole = lax.dot_general(
            mixed, delta, (((0,), (0,)), ((), ())), preferred_element_type=jnp.float32
        )
        return whole.reshape(depth, shards, depth // shards).transpose(1, 2, 0)

    def reduce_blocks(parts):
        me = lax.axis_index(AXES)
        step = 1
        while step < shards:
            held = parts.shape[1]
            pair = parts.reshape(parts.shape[0], held // 2, 2, *parts.shape[2:])
            upper = (me // step) % 2 == 1
            keep = jnp.where(upper, pair[:, :, 1], pair[:, :, 0])
            send = jnp.where(upper, pair[:, :, 0], pair[:, :, 1])
            if step > 1:
                send = send.astype(jnp.bfloat16)
            moved = lax.ppermute(send, AXES, [(i, i ^ step) for i in range(shards)])
            parts = keep + moved.astype(jnp.float32)
            step *= 2
        return parts[:, 0] / (groups * shards)

    mixed_one, first_matmul_result, _ = forward_layer(None, whole_weight_one, spread_in)
    latent_state = (
        jax.nn.silu(first_matmul_result).astype(jnp.bfloat16).reshape(groups, width, depth)
    )
    mixed_two, product_two, _ = forward_layer(latent_state, whole_weight_two)
    delta_two = (
        final_layer_sensitivity.reshape(count, depth).astype(jnp.float32) * swish_slope(product_two)
    ).astype(jnp.bfloat16)
    parts_two = grad_parts(mixed_two, delta_two)
    upstream_second = back_weight(delta_two, whole_weight_two)
    fetched_second = (normalizer_factor * upstream_second.reshape(groups, width, depth)).astype(
        jnp.bfloat16
    )
    delta_one = (
        spread_back(link, fetched_second).reshape(count, depth) * swish_slope(first_matmul_result)
    ).astype(jnp.bfloat16)
    parts_one = grad_parts(mixed_one, delta_one)
    upstream_first = back_weight(delta_one, whole_weight_one)
    fetched_first = (normalizer_factor * upstream_first.reshape(groups, width, depth)).astype(
        jnp.bfloat16
    )
    outgoing = lax.dot_general(
        linked_slots,
        fetched_first.reshape(count, depth),
        (((0,), (0,)), ((), ())),
        preferred_element_type=jnp.float32,
    ).astype(jnp.bfloat16)
    returned = exchange(outgoing)
    table_grad = lax.dot_general(
        picks, returned, (((0, 1), (0, 1)), ((), ())), preferred_element_type=jnp.float32
    )
    grad_one = reduce_blocks(parts_one[None])[0].T
    grad_two = reduce_blocks(parts_two[None])[0].T
    return (table_grad, grad_one, grad_two)


def solution(mesh):
    placed = (
        P(AXES, None),
        P(AXES, None),
        P(AXES, None, None),
        P(None, "fsdp"),
        P(None, "fsdp"),
        P(AXES, None, None),
    )
    return jax.shard_map(
        step_body,
        mesh=mesh,
        in_specs=placed,
        out_specs=(P(AXES, None), P(None, AXES), P(None, AXES)),
        check_vma=False,
    )
```

```python
import jax
import jax.numpy as jnp
from jax import lax
from jax.sharding import PartitionSpec as P

AXES = ("node", "fsdp")


def swish_slope(values):
    sigma = jax.nn.sigmoid(values)
    return sigma * (1.0 + values * (1.0 - sigma))


def spread(link, values):
    return jnp.einsum("gij,gjd->gid", link, values, preferred_element_type=jnp.float32)


def spread_back(link, values):
    return jnp.einsum("gji,gjd->gid", link, values, preferred_element_type=jnp.float32)


def exchange(values):
    return lax.all_to_all(values, AXES, 0, 0, tiled=True)


def step_body(
    feature_table, vertex_labels, incidence_mask, weight_one, weight_two, final_layer_sensitivity
):
    groups, width = vertex_labels.shape
    count = groups * width
    n_node = lax.axis_size("node")
    n_fsdp = lax.axis_size("fsdp")
    shards = n_node * n_fsdp
    rows_here = feature_table.shape[0]
    depth = feature_table.shape[1]
    capacity = (2 * count + shards - 1) // shards + 1
    flat_ids = vertex_labels.reshape(count)
    owner = flat_ids // rows_here
    within = flat_ids % rows_here
    one_hot = (owner[:, None] == jnp.arange(shards, dtype=jnp.int32)[None, :]).astype(jnp.int32)
    before = jnp.cumsum(one_hot, axis=0) - one_hot
    rank = jnp.sum(before * one_hot, axis=1)
    position = owner * capacity + rank
    requests = jnp.full((shards * capacity,), -1, jnp.int32).at[position].set(within)
    asked = exchange(requests.reshape(shards, capacity))
    valid = asked >= 0
    safe_rows = jnp.maximum(asked, 0)
    picks = (
        (safe_rows[..., None] == jnp.arange(rows_here, dtype=jnp.int32)) & valid[..., None]
    ).astype(jnp.bfloat16)
    found = jnp.dot(picks, feature_table, preferred_element_type=jnp.float32).astype(jnp.bfloat16)
    answered = exchange(found)
    slot_of = (
        (owner[:, None, None] == jnp.arange(shards, dtype=jnp.int32)[:, None])
        & (rank[:, None, None] == jnp.arange(capacity, dtype=jnp.int32))
    ).astype(jnp.bfloat16)
    degree = jnp.sum(incidence_mask, axis=2).astype(jnp.float32)
    normalizer_factor = lax.rsqrt(1.0 + degree)[..., None]
    link = (incidence_mask + jnp.eye(width, dtype=jnp.int32)[None]).astype(jnp.bfloat16)
    linked_slots = (
        jnp.einsum(
            "gij,gjsc->gisc",
            link,
            slot_of.reshape(groups, width, shards, capacity),
            preferred_element_type=jnp.float32,
        )
        .astype(jnp.bfloat16)
        .reshape(count, shards, capacity)
    )
    spread_in = lax.dot_general(
        linked_slots, answered, (((1, 2), (0, 1)), ((), ())), preferred_element_type=jnp.float32
    )

    def forward_layer(layer_in, weight, spread_done=None):
        if spread_done is None:
            spread_done = spread(link, layer_in)
        mixed = (
            (normalizer_factor * spread_done.reshape(groups, width, depth))
            .astype(jnp.bfloat16)
            .reshape(count, depth)
        )
        product = jnp.dot(mixed, weight, preferred_element_type=jnp.float32)
        return (mixed, product, weight)

    def back_weight(delta, weight):
        return lax.dot_general(
            delta, weight, (((1,), (1,)), ((), ())), preferred_element_type=jnp.float32
        )

    def gather_columns(weight):
        column = lax.axis_index("fsdp")
        blocks = weight[None]
        step = n_fsdp // 2
        while step >= 1:
            other = lax.ppermute(blocks, "fsdp", [(i, i ^ step) for i in range(n_fsdp)])
            upper = (column // step) % 2 == 1
            blocks = jnp.concatenate(
                [jnp.where(upper, other, blocks), jnp.where(upper, blocks, other)], axis=0
            )
            step //= 2
        bits = n_fsdp.bit_length() - 1
        blocks = blocks.reshape((2,) * bits + weight.shape)
        blocks = blocks.transpose(tuple(range(bits))[::-1] + (bits, bits + 1))
        blocks = blocks.reshape((n_fsdp,) + weight.shape)
        return blocks.transpose(1, 0, 2).reshape(weight.shape[0], n_fsdp * weight.shape[1])

    whole_weight_one = gather_columns(weight_one)
    whole_weight_two = gather_columns(weight_two)

    def grad_parts(mixed, delta):
        whole = lax.dot_general(
            mixed, delta, (((0,), (0,)), ((), ())), preferred_element_type=jnp.float32
        )
        return whole.reshape(depth, shards, depth // shards).transpose(1, 2, 0)

    def reduce_blocks(parts):
        me = lax.axis_index(AXES)
        step = 1
        while step < shards:
            held = parts.shape[1]
            pair = parts.reshape(parts.shape[0], held // 2, 2, *parts.shape[2:])
            upper = (me // step) % 2 == 1
            keep = jnp.where(upper, pair[:, :, 1], pair[:, :, 0])
            send = jnp.where(upper, pair[:, :, 0], pair[:, :, 1])
            if step > 1:
                send = send.astype(jnp.bfloat16)
            moved = lax.ppermute(send, AXES, [(i, i ^ step) for i in range(shards)])
            parts = keep + moved.astype(jnp.float32)
            step *= 2
        return parts[:, 0] / (groups * shards)

    mixed_one, first_matmul_result, _ = forward_layer(None, whole_weight_one, spread_in)
    latent_state = (
        jax.nn.silu(first_matmul_result).astype(jnp.bfloat16).reshape(groups, width, depth)
    )
    mixed_two, product_two, _ = forward_layer(latent_state, whole_weight_two)
    delta_two = (
        final_layer_sensitivity.reshape(count, depth).astype(jnp.float32) * swish_slope(product_two)
    ).astype(jnp.bfloat16)
    parts_two = grad_parts(mixed_two, delta_two)
    upstream_second = back_weight(delta_two, whole_weight_two)
    fetched_second = (normalizer_factor * upstream_second.reshape(groups, width, depth)).astype(
        jnp.bfloat16
    )
    delta_one = (
        spread_back(link, fetched_second).reshape(count, depth) * swish_slope(first_matmul_result)
    ).astype(jnp.bfloat16)
    parts_one = grad_parts(mixed_one, delta_one)
    upstream_first = back_weight(delta_one, whole_weight_one)
    fetched_first = (normalizer_factor * upstream_first.reshape(groups, width, depth)).astype(
        jnp.bfloat16
    )
    slots_linked = jnp.einsum(
        "gij,gjsc->scgi",
        link,
        slot_of.reshape(groups, width, shards, capacity),
        preferred_element_type=jnp.float32,
    ).astype(jnp.bfloat16)
    outgoing = lax.dot_general(
        slots_linked.reshape(shards, capacity, count),
        fetched_first.reshape(count, depth),
        (((2,), (0,)), ((), ())),
        preferred_element_type=jnp.float32,
    ).astype(jnp.bfloat16)
    returned = exchange(outgoing)
    table_grad = lax.dot_general(
        picks, returned, (((0, 1), (0, 1)), ((), ())), preferred_element_type=jnp.float32
    )
    grad_one = reduce_blocks(parts_one[None])[0].T
    grad_two = reduce_blocks(parts_two[None])[0].T
    return (table_grad, grad_one, grad_two)


def solution(mesh):
    placed = (
        P(AXES, None),
        P(AXES, None),
        P(AXES, None, None),
        P(None, "fsdp"),
        P(None, "fsdp"),
        P(AXES, None, None),
    )
    return jax.shard_map(
        step_body,
        mesh=mesh,
        in_specs=placed,
        out_specs=(P(AXES, None), P(None, AXES), P(None, AXES)),
        check_vma=False,
    )
```

```python
import jax
import jax.numpy as jnp
from jax import lax
from jax.sharding import PartitionSpec as P

AXES = ("node", "fsdp")


def swish_slope(values):
    sigma = jax.nn.sigmoid(values)
    return sigma * (1.0 + values * (1.0 - sigma))


def spread(link, values):
    return jnp.einsum("gij,gjd->gid", link, values, preferred_element_type=jnp.float32)


def spread_back(link, values):
    return jnp.einsum("gji,gjd->gid", link, values, preferred_element_type=jnp.float32)


def exchange(values):
    return lax.all_to_all(values, AXES, 0, 0, tiled=True)


def step_body(
    feature_table, vertex_labels, incidence_mask, weight_one, weight_two, final_layer_sensitivity
):
    groups, width = vertex_labels.shape
    count = groups * width
    n_node = lax.axis_size("node")
    n_fsdp = lax.axis_size("fsdp")
    shards = n_node * n_fsdp
    rows_here = feature_table.shape[0]
    depth = feature_table.shape[1]
    capacity = (2 * count + shards - 1) // shards + 1
    flat_ids = vertex_labels.reshape(count)
    owner = flat_ids // rows_here
    within = flat_ids % rows_here
    one_hot = (owner[:, None] == jnp.arange(shards, dtype=jnp.int32)[None, :]).astype(jnp.int32)
    before = jnp.cumsum(one_hot, axis=0) - one_hot
    rank = jnp.sum(before * one_hot, axis=1)
    position = owner * capacity + rank
    requests = jnp.full((shards * capacity,), -1, jnp.int32).at[position].set(within)
    asked = exchange(requests.reshape(shards, capacity))
    valid = asked >= 0
    safe_rows = jnp.maximum(asked, 0)
    picks = (
        (safe_rows[..., None] == jnp.arange(rows_here, dtype=jnp.int32)) & valid[..., None]
    ).astype(jnp.bfloat16)
    found = jnp.dot(picks, feature_table, preferred_element_type=jnp.float32).astype(jnp.bfloat16)
    answered = exchange(found)
    slot_of = (
        (owner[:, None, None] == jnp.arange(shards, dtype=jnp.int32)[:, None])
        & (rank[:, None, None] == jnp.arange(capacity, dtype=jnp.int32))
    ).astype(jnp.bfloat16)
    degree = jnp.sum(incidence_mask, axis=2).astype(jnp.float32)
    normalizer_factor = lax.rsqrt(1.0 + degree)[..., None]
    link = (incidence_mask + jnp.eye(width, dtype=jnp.int32)[None]).astype(jnp.bfloat16)
    linked_slots = (
        jnp.einsum(
            "gij,gjsc->gisc",
            link,
            slot_of.reshape(groups, width, shards, capacity),
            preferred_element_type=jnp.float32,
        )
        .astype(jnp.bfloat16)
        .reshape(count, shards, capacity)
    )
    spread_in = lax.dot_general(
        linked_slots, answered, (((1, 2), (0, 1)), ((), ())), preferred_element_type=jnp.float32
    )

    def forward_layer(layer_in, weight, spread_done=None):
        if spread_done is None:
            spread_done = spread(link, layer_in)
        mixed = (
            (normalizer_factor * spread_done.reshape(groups, width, depth))
            .astype(jnp.bfloat16)
            .reshape(count, depth)
        )
        product = jnp.dot(mixed, weight, preferred_element_type=jnp.float32)
        return (mixed, product, weight)

    def back_weight(delta, weight):
        return lax.dot_general(
            delta, weight, (((1,), (1,)), ((), ())), preferred_element_type=jnp.float32
        )

    def gather_columns(weight):
        column = lax.axis_index("fsdp")
        blocks = weight[None]
        step = n_fsdp // 2
        while step >= 1:
            other = lax.ppermute(blocks, "fsdp", [(i, i ^ step) for i in range(n_fsdp)])
            upper = (column // step) % 2 == 1
            blocks = jnp.concatenate(
                [jnp.where(upper, other, blocks), jnp.where(upper, blocks, other)], axis=0
            )
            step //= 2
        bits = n_fsdp.bit_length() - 1
        blocks = blocks.reshape((2,) * bits + weight.shape)
        blocks = blocks.transpose(tuple(range(bits))[::-1] + (bits, bits + 1))
        blocks = blocks.reshape((n_fsdp,) + weight.shape)
        return blocks.transpose(1, 0, 2).reshape(weight.shape[0], n_fsdp * weight.shape[1])

    whole_weight_one = gather_columns(weight_one)
    whole_weight_two = gather_columns(weight_two)

    def grad_parts(mixed, delta):
        whole = lax.dot_general(
            mixed, delta, (((0,), (0,)), ((), ())), preferred_element_type=jnp.float32
        )
        return whole.reshape(depth, shards, depth // shards).transpose(1, 2, 0)

    def reduce_blocks(parts):
        me = lax.axis_index(AXES)
        step = 1
        while step < shards:
            held = parts.shape[1]
            pair = parts.reshape(parts.shape[0], held // 2, 2, *parts.shape[2:])
            upper = (me // step) % 2 == 1
            keep = jnp.where(upper, pair[:, :, 1], pair[:, :, 0])
            send = jnp.where(upper, pair[:, :, 0], pair[:, :, 1])
            if step > 1:
                send = send.astype(jnp.bfloat16)
            moved = lax.ppermute(send, AXES, [(i, i ^ step) for i in range(shards)])
            parts = keep + moved.astype(jnp.float32)
            step *= 2
        return parts[:, 0] / (groups * shards)

    mixed_one, first_matmul_result, _ = forward_layer(None, whole_weight_one, spread_in)
    latent_state = (
        jax.nn.silu(first_matmul_result).astype(jnp.bfloat16).reshape(groups, width, depth)
    )
    mixed_two, product_two, _ = forward_layer(latent_state, whole_weight_two)
    delta_two = (
        final_layer_sensitivity.reshape(count, depth).astype(jnp.float32) * swish_slope(product_two)
    ).astype(jnp.bfloat16)
    parts_two = grad_parts(mixed_two, delta_two)
    upstream_second = back_weight(delta_two, whole_weight_two)
    fetched_second = (normalizer_factor * upstream_second.reshape(groups, width, depth)).astype(
        jnp.bfloat16
    )
    delta_one = (
        spread_back(link, fetched_second).reshape(count, depth) * swish_slope(first_matmul_result)
    ).astype(jnp.bfloat16)
    parts_one = grad_parts(mixed_one, delta_one)
    upstream_first = back_weight(delta_one, whole_weight_one)
    fetched_first = (normalizer_factor * upstream_first.reshape(groups, width, depth)).astype(
        jnp.bfloat16
    )
    outgoing = lax.dot_general(
        linked_slots,
        fetched_first.reshape(count, depth),
        (((0,), (0,)), ((), ())),
        preferred_element_type=jnp.float32,
    ).astype(jnp.bfloat16)
    returned = exchange(outgoing)
    picked_rows = (
        (jnp.arange(rows_here, dtype=jnp.int32)[:, None, None] == safe_rows) & valid
    ).astype(jnp.bfloat16)
    table_grad = lax.dot_general(
        picked_rows,
        returned,
        (((1, 2), (0, 1)), ((), ())),
        preferred_element_type=jnp.float32,
    )
    grad_one = reduce_blocks(parts_one[None])[0].T
    grad_two = reduce_blocks(parts_two[None])[0].T
    return (table_grad, grad_one, grad_two)


def solution(mesh):
    placed = (
        P(AXES, None),
        P(AXES, None),
        P(AXES, None, None),
        P(None, "fsdp"),
        P(None, "fsdp"),
        P(AXES, None, None),
    )
    return jax.shard_map(
        step_body,
        mesh=mesh,
        in_specs=placed,
        out_specs=(P(AXES, None), P(None, AXES), P(None, AXES)),
        check_vma=False,
    )
```
